512 devices in a mesh: dp: 8 (over y, core), tensor: 64 (over x, z).
Axes of the slice: x: 4, y: 4, z: 16, core: 2. Of those that a mesh axis runs over, the one named last changes fastest.
Arguments:
- tokens: bfloat16 [8, 128, 4544], P('dp', 'tensor'), may hold values from -6 to 6
- ln_gain: float32 [4544], replicated, may hold values from 0.1 to 1.9
- ln_bias: float32 [4544], replicated, may hold values from -3 to 3
- q_weight: bfloat16 [4544, 4096], P(None, 'tensor'), may hold values from -0.09375 to 0.09375
- kv_weight: bfloat16 [4544, 128], replicated, may hold values from -0.25 to 0.25
- dense_weight: bfloat16 [4096, 4544], P('tensor'), may hold values from -0.09375 to 0.09375
- up_weight: bfloat16 [4544, 9088], P(None, 'tensor'), may hold values from -0.09375 to 0.09375
- down_weight: bfloat16 [9088, 4544], P('tensor'), may hold values from -0.0625 to 0.0625
- kv_cache: bfloat16 [8, 512, 64, 128], P(None, 'tensor', 'dp'), may hold values from -96 to 96
- cache_lengths: int32 [8], replicated, may hold values from 512 to 32768, as said below
Outputs:
- layer_out: bfloat16 [8, 128, 4544], P('dp', 'tensor')
The draws below stay inside these ranges and needn't reach their ends.
Inputs may be any that keep to these rules, and one draw needn't show every extreme that they name: `cache_lengths`: exactly one request has 32768 cached positions; each other has between 512 and 2048.
All inputs are finite; a program needn't handle non-finite values.
Results may differ from the reference program's by a relative error of at most 0.04.
Values may be sent and summed in bfloat16 or wider, within the bound.
No kernel may reach another device: no remote copies, remote signals or barrier semaphores. Data moves between devices by JAX's collectives and lax.ppermute only.
A program may use at most 128 MiB of HBM per device.

```python
import math
import jax
import jax.numpy as jnp
from jax import lax

D = 4544
HD = 64
HEADS = 64
FF = 9088
SPAN = 128
REQUESTS = 8
HQ = 4096
INNER = 64
OUTER = 512
CACHE_MAX = 32768


def draw_kv_cache(key, part):
    shape = (REQUESTS, OUTER, INNER, 2 * HD)
    first_key = jax.random.fold_in(key, 0)
    values = jnp.clip(3.0 * jax.random.normal(first_key, shape, jnp.float32), -15.0, 15.0)
    return values.astype(jnp.bfloat16)


def draw_cache_lengths(key, part):
    first_key, second_key = jax.random.split(key)
    short = jax.random.randint(first_key, (REQUESTS,), CACHE_MAX // 64, CACHE_MAX // 16 + 1)
    which = jax.random.randint(second_key, (), 0, REQUESTS)
    return jnp.where(jnp.arange(REQUESTS) == which, CACHE_MAX, short).astype(jnp.int32)


def block_scale(key, shape, cuts, least, largest):
    def one(position, shards_of):
        draws = jax.random.uniform(jax.random.fold_in(jax.random.fold_in(key, 6), position), (shards_of,), jnp.float32, least / len(cuts), largest / len(cuts))
        return jnp.repeat(jnp.exp(draws), shape[position] // shards_of).reshape((-1,) + (1,) * (len(shape) - position - 1))

    level = one(*cuts[0])
    for cut in cuts[1:]:
        level = level * one(*cut)
    return level


def bell_draw(own_key, dims, spread, bound, cuts=(), kind=jnp.bfloat16):
    array = jax.random.normal(own_key, dims, jnp.float32) * spread
    if len(cuts) > 0:
        array = block_scale(own_key, dims, cuts, -0.22, 0.18) * array
    return jnp.clip(array, min=-bound, max=bound).astype(kind)


def setup_inputs(seed: int = 0) -> dict:
    key_of = jax.random.split(jax.random.key(seed), 11)
    return {
        "tokens": bell_draw(key_of[0], (REQUESTS, SPAN, D), 1.0, 6.0, ((0, 8), (1, 64))),
        "ln_gain": jnp.clip(1.0 + 0.18 * jax.random.normal(key_of[1], (D,), jnp.float32), 0.1, 1.9),
        "ln_bias": bell_draw(key_of[2], (D,), 0.5, 3.0, (), jnp.float32),
        "q_weight": bell_draw(key_of[3], (D, HQ), D ** -0.5, 0.09375, ((1, 64),)),
        "kv_weight": bell_draw(key_of[4], (D, 2 * HD), (D // 9) ** -0.5, 0.25),
        "dense_weight": bell_draw(key_of[5], (HQ, D), HQ ** -0.5, 0.09375, ((0, 64),)),
        "up_weight": bell_draw(key_of[6], (D, FF), D ** -0.5, 0.09375, ((1, 64),)),
        "down_weight": bell_draw(key_of[7], (FF, D), FF ** -0.5, 0.0625, ((0, 64),)),
        "kv_cache": draw_kv_cache(jax.random.fold_in(key_of[10], 71), 0),
        "cache_lengths": draw_cache_lengths(jax.random.fold_in(key_of[10], 71), 0),
    }


NEGATIVE = -1e+30

def norm_rows(rows, gain, shift):
    widened = rows.astype(jnp.float32)
    center = lax.optimization_barrier(jnp.mean(widened, axis=-1, keepdims=True))
    centered = widened - center
    variance = lax.optimization_barrier(jnp.mean(centered * centered, axis=-1, keepdims=True))
    return (centered * lax.rsqrt(variance + 1e-05) * gain + shift).astype(jnp.bfloat16)

def rotary_tables(places, width):
    half = width // 2
    freqs = jnp.exp(jnp.arange(half, dtype=jnp.float32) * (-2.0 * math.log(10000.0) / width))
    angle = places.astype(jnp.float32)[..., None] * freqs
    cosine = jnp.concatenate([jnp.cos(angle), jnp.cos(angle)], axis=-1)
    sine = jnp.concatenate([jnp.sin(angle), jnp.sin(angle)], axis=-1)
    return (cosine, sine)

def rotate(values, cosine, sine):
    half = values.shape[-1] // 2
    turned = jnp.concatenate([-values[..., half:], values[..., :half]], axis=-1)
    return values * cosine + turned * sine

def combine(first, second):
    first_values, first_top, first_total = first
    second_values, second_top, second_total = second
    best = jnp.maximum(first_top, second_top)
    first_scale = jnp.exp(first_top - best)
    second_scale = jnp.exp(second_top - best)
    return (first_values * first_scale[..., None] + second_values * second_scale[..., None], best, first_total * first_scale + second_total * second_scale)

def absorb(state, queries, key_rows, value_rows, valid):
    scores = jnp.dot(queries, key_rows.T, preferred_element_type=jnp.float32) * (1.0 / math.sqrt(queries.shape[-1]))
    scores = jnp.where(valid, scores, NEGATIVE)
    best = lax.optimization_barrier(jnp.max(scores, axis=1))
    weights = jnp.exp(scores - best[:, None])
    block = (jnp.dot(weights.astype(jnp.bfloat16), value_rows, preferred_element_type=jnp.float32), best, lax.optimization_barrier(jnp.sum(weights, axis=1)))
    return combine(state, block)

def empty_state(rows, width):
    return (jnp.zeros((rows, width), jnp.float32), jnp.full((rows,), NEGATIVE, jnp.float32), jnp.zeros((rows,), jnp.float32))

def reference(tokens, ln_gain, ln_bias, q_weight, kv_weight, dense_weight, up_weight, down_weight, kv_cache, cache_lengths):
    requests, span, width_model = tokens.shape
    normed = norm_rows(tokens, ln_gain, ln_bias)
    flat = normed.reshape(requests * span, width_model)
    query_all = jnp.dot(flat, q_weight, preferred_element_type=jnp.float32).reshape(requests, span, HEADS, HD)
    key_value = jnp.dot(flat, kv_weight, preferred_element_type=jnp.float32).reshape(requests, span, 2 * HD)
    hidden = jax.nn.gelu(jnp.dot(flat, up_weight, preferred_element_type=jnp.float32), approximate=False).astype(jnp.bfloat16)
    places = cache_lengths[:, None] + jnp.arange(span, dtype=jnp.int32)[None, :]
    cosine, sine = rotary_tables(places, HD)
    queries = rotate(query_all, cosine[:, :, None, :], sine[:, :, None, :]).reshape(requests, span * HEADS, HD).astype(jnp.bfloat16)
    new_keys = rotate(key_value[..., :HD], cosine, sine).astype(jnp.bfloat16)
    new_values = key_value[..., HD:].astype(jnp.bfloat16)
    cache = kv_cache.reshape(requests, CACHE_MAX, 2 * HD)
    block = math.gcd(CACHE_MAX, 512)
    blocks = CACHE_MAX // block
    rows = span * HEADS

    def one_request(inputs):
        query_rows, keys_all, length, fresh_keys, fresh_values = inputs

        def step(state, index):
            start = index * block
            keys = lax.dynamic_slice_in_dim(keys_all, start, block, 0)
            places_block = start + jnp.arange(block, dtype=jnp.int32)
            valid = (places_block < length)[None, :]
            updated = lax.cond(start < length, lambda carry: absorb(carry, query_rows, keys[:, :HD], keys[:, HD:], valid), lambda carry: carry, state)
            return (updated, None)
        state, _ = lax.scan(step, empty_state(rows, HD), jnp.arange(blocks, dtype=jnp.int32))
        token_of_row = jnp.arange(rows, dtype=jnp.int32) // HEADS
        causal = jnp.arange(span, dtype=jnp.int32)[None, :] <= token_of_row[:, None]
        summed, best, total = absorb(state, query_rows, fresh_keys, fresh_values, causal)
        return summed / total[:, None]
    attn = lax.map(one_request, (queries, cache, cache_lengths, new_keys, new_values))
    attn = attn.reshape(requests * span, HQ).astype(jnp.bfloat16)
    mixed = jnp.dot(attn, dense_weight, preferred_element_type=jnp.float32) + jnp.dot(hidden, down_weight, preferred_element_type=jnp.float32)
    result = tokens.reshape(requests * span, width_model).astype(jnp.float32) + mixed
    return result.astype(jnp.bfloat16).reshape(requests, span, width_model)
```

```python
import math

import jax
import jax.numpy as jnp
from jax import lax
from jax.sharding import Mesh
from jax.sharding import PartitionSpec as P

NEGATIVE = -1e30
TENSOR = ("tx", "tz")


def norm_rows(rows, gain, shift):
    widened = rows.astype(jnp.float32)
    center = jnp.mean(widened, axis=-1, keepdims=True)
    centered = widened - center
    variance = jnp.mean(centered * centered, axis=-1, keepdims=True)
    return (centered * lax.rsqrt(variance + 1e-05) * gain + shift).astype(jnp.bfloat16)


def rotary_tables(places, width):
    half = width // 2
    freqs = jnp.exp(jnp.arange(half, dtype=jnp.float32) * (-2.0 * math.log(10000.0) / width))
    angle = places.astype(jnp.float32)[..., None] * freqs
    cosine = jnp.concatenate([jnp.cos(angle), jnp.cos(angle)], axis=-1)
    sine = jnp.concatenate([jnp.sin(angle), jnp.sin(angle)], axis=-1)
    return (cosine, sine)


def rotate(values, cosine, sine):
    half = values.shape[-1] // 2
    turned = jnp.concatenate([-values[..., half:], values[..., :half]], axis=-1)
    return values * cosine + turned * sine


def combine(first, second):
    first_values, first_top, first_total = first
    second_values, second_top, second_total = second
    best = jnp.maximum(first_top, second_top)
    first_scale = jnp.exp(first_top - best)
    second_scale = jnp.exp(second_top - best)
    return (
        first_values * first_scale[..., None] + second_values * second_scale[..., None],
        best,
        first_total * first_scale + second_total * second_scale,
    )


def absorb(state, queries, key_rows, value_rows, valid):
    scores = jnp.dot(queries, key_rows.T, preferred_element_type=jnp.float32) * (
        1.0 / math.sqrt(queries.shape[-1])
    )
    scores = jnp.where(valid, scores, NEGATIVE)
    best = jnp.max(scores, axis=1)
    weights = jnp.exp(scores - best[:, None])
    block = (
        jnp.dot(weights.astype(jnp.bfloat16), value_rows, preferred_element_type=jnp.float32),
        best,
        jnp.sum(weights, axis=1),
    )
    return combine(state, block)


def fold_keys(state, queries, keys, valid):
    width = queries.shape[-1]
    return absorb(state, queries, keys[:, :width], keys[:, width:], valid)


def empty_state(rows, width, lead):
    return (
        jnp.zeros(lead + (rows, width), jnp.float32),
        jnp.full(lead + (rows,), NEGATIVE, jnp.float32),
        jnp.zeros(lead + (rows,), jnp.float32),
    )


def tensor_index():
    return lax.axis_index("tx") * lax.axis_size("tz") + lax.axis_index("tz")


def bit_reversed(index, bits):
    out = jnp.zeros_like(index)
    for b in range(bits):
        out = out | (((index >> b) & 1) << (bits - 1 - b))
    return out


def gather_rounds(piece, n):
    bits = n.bit_length() - 1
    me = tensor_index()
    buf = piece[None]
    for b in reversed(range(bits)):
        other = lax.ppermute(buf, TENSOR, [(i, i ^ (1 << b)) for i in range(n)])
        low = ((me >> b) & 1) == 0
        buf = jnp.concatenate(
            [jnp.where(low, buf, other), jnp.where(low, other, buf)], axis=0
        )
    return buf


def scatter_rounds(partial, n):
    bits = n.bit_length() - 1
    me = tensor_index()
    buf = partial.reshape((2,) * bits + partial.shape[1:])
    for b in range(bits):
        mine = (me >> b) & 1
        keep = lax.dynamic_index_in_dim(buf, mine, 0, keepdims=False)
        send = lax.dynamic_index_in_dim(buf, 1 - mine, 0, keepdims=False)
        buf = keep + lax.ppermute(send, TENSOR, [(i, i ^ (1 << b)) for i in range(n)])
    return buf


def local(
    tokens,
    ln_gain,
    ln_bias,
    q_weight,
    kv_weight,
    dense_weight,
    up_weight,
    down_weight,
    kv_cache,
    cache_lengths,
):
    n = lax.axis_size("tx") * lax.axis_size("tz")
    bits = n.bit_length() - 1
    width = kv_weight.shape[1] // 2
    query_cols = q_weight.shape[1]
    heads_here = query_cols // width
    width_model = tokens.shape[-1]
    per_device = tokens.shape[1]

    mine = lax.all_to_all(kv_cache, "dp", split_axis=0, concat_axis=2, tiled=True)
    inner_all = mine.shape[2]
    gathered = lax.all_gather(mine, "tz", axis=1, tiled=True)
    gathered = lax.all_gather(gathered, "tx", axis=1, tiled=True)
    flat_keys = gathered[0].reshape(-1, 2 * width)

    normed = norm_rows(tokens[0], ln_gain, ln_bias)
    piece = gather_rounds(normed, n).reshape(n * per_device, width_model)
    projected = jnp.concatenate(
        [
            jnp.dot(piece, q_weight, preferred_element_type=jnp.float32),
            jnp.dot(piece, kv_weight, preferred_element_type=jnp.float32),
            jnp.dot(piece, up_weight, preferred_element_type=jnp.float32),
        ],
        axis=1,
    )
    span = projected.shape[0]
    row = jnp.arange(span, dtype=jnp.int32)
    token_pos = bit_reversed(row // per_device, bits) * per_device + row % per_device
    group = lax.axis_index("dp")
    own_length = lax.dynamic_index_in_dim(cache_lengths, group, 0, keepdims=False)
    places = own_length + token_pos
    cosine, sine = rotary_tables(places, width)
    queries = rotate(
        projected[:, :query_cols].reshape(span, heads_here, width),
        cosine[:, None, :],
        sine[:, None, :],
    ).astype(jnp.bfloat16)
    new_keys = rotate(projected[:, query_cols : query_cols + width], cosine, sine).astype(
        jnp.bfloat16
    )
    new_values = projected[:, query_cols + width : query_cols + 2 * width].astype(jnp.bfloat16)
    hidden = jax.nn.gelu(projected[:, query_cols + 2 * width :], approximate=False).astype(
        jnp.bfloat16
    )
    rows = span * heads_here
    query_rows = queries.reshape(rows, width)
    places_piece = jnp.arange(flat_keys.shape[0], dtype=jnp.int32)
    valid = (places_piece < own_length)[None, :]
    state = lax.cond(
        jnp.int32(0) * inner_all < own_length,
        lambda carry: fold_keys(carry, query_rows, flat_keys, valid),
        lambda carry: carry,
        empty_state(rows, width, ()),
    )
    pos_of_row = jnp.repeat(token_pos, heads_here)
    causal = token_pos[None, :] <= pos_of_row[:, None]
    summed, best, total = absorb(state, query_rows, new_keys, new_values, causal)
    attn = (summed / total[:, None]).astype(jnp.bfloat16)
    partial = jnp.dot(attn, dense_weight, preferred_element_type=jnp.float32) + jnp.dot(
        hidden, down_weight, preferred_element_type=jnp.float32
    )
    layer_rows = scatter_rounds(partial.reshape(n, per_device, width_model), n)
    return (tokens[0].astype(jnp.float32) + layer_rows).astype(jnp.bfloat16)[None]


def solution(mesh):
    dp = mesh.shape["dp"]
    tensor = mesh.shape["tensor"]
    tx = 4 if tensor % 4 == 0 else 1
    mesh3 = Mesh(mesh.devices.reshape(dp, tx, tensor // tx), ("dp", "tx", "tz"))
    return jax.shard_map(
        local,
        mesh=mesh3,
        in_specs=(
            P("dp", TENSOR, None),
            P(),
            P(),
            P(None, TENSOR),
            P(),
            P(TENSOR, None),
            P(None, TENSOR),
            P(TENSOR, None),
            P(None, TENSOR, "dp", None),
            P(),
        ),
        out_specs=P("dp", TENSOR, None),
        check_vma=False,
    )
```

```python
import math

import jax
import jax.numpy as jnp
from jax import lax
from jax.sharding import Mesh
from jax.sharding import PartitionSpec as P

NEGATIVE = -1e30
TENSOR = ("tx", "tz")


def norm_rows(rows, gain, shift):
    widened = rows.astype(jnp.float32)
    center = jnp.mean(widened, axis=-1, keepdims=True)
    centered = widened - center
    variance = jnp.mean(centered * centered, axis=-1, keepdims=True)
    return (centered * lax.rsqrt(variance + 1e-05) * gain + shift).astype(jnp.bfloat16)


def rotary_tables(places, width):
    half = width // 2
    freqs = jnp.exp(jnp.arange(half, dtype=jnp.float32) * (-2.0 * math.log(10000.0) / width))
    angle = places.astype(jnp.float32)[..., None] * freqs
    cosine = jnp.concatenate([jnp.cos(angle), jnp.cos(angle)], axis=-1)
    sine = jnp.concatenate([jnp.sin(angle), jnp.sin(angle)], axis=-1)
    return (cosine, sine)


def rotate(values, cosine, sine):
    half = values.shape[-1] // 2
    turned = jnp.concatenate([-values[..., half:], values[..., :half]], axis=-1)
    return values * cosine + turned * sine


def combine(first, second):
    first_values, first_top, first_total = first
    second_values, second_top, second_total = second
    best = jnp.maximum(first_top, second_top)
    first_scale = jnp.exp(first_top - best)
    second_scale = jnp.exp(second_top - best)
    return (
        first_values * first_scale[..., None] + second_values * second_scale[..., None],
        best,
        first_total * first_scale + second_total * second_scale,
    )


def absorb(state, queries, key_rows, value_rows, valid):
    scores = jnp.dot(queries, key_rows.T, preferred_element_type=jnp.float32) * (
        1.0 / math.sqrt(queries.shape[-1])
    )
    scores = jnp.where(valid, scores, NEGATIVE)
    best = jnp.max(scores, axis=1)
    weights = jnp.exp(scores - best[:, None])
    block = (
        jnp.dot(weights.astype(jnp.bfloat16), value_rows, preferred_element_type=jnp.float32),
        best,
        jnp.sum(weights, axis=1),
    )
    return combine(state, block)


def fold_keys(state, queries, keys, valid):
    width = queries.shape[-1]
    return absorb(state, queries, keys[:, :width], keys[:, width:], valid)


def empty_state(rows, width, lead):
    return (
        jnp.zeros(lead + (rows, width), jnp.float32),
        jnp.full(lead + (rows,), NEGATIVE, jnp.float32),
        jnp.zeros(lead + (rows,), jnp.float32),
    )


def tensor_index():
    return lax.axis_index("tx") * lax.axis_size("tz") + lax.axis_index("tz")


def bit_reversed(index, bits):
    out = jnp.zeros_like(index)
    for b in range(bits):
        out = out | (((index >> b) & 1) << (bits - 1 - b))
    return out


def round_bits(n):
    bits = n.bit_length() - 1
    low = lax.axis_size("tz").bit_length() - 1
    return list(reversed(range(low))) + list(reversed(range(low, bits)))


def layout_source(index, n):
    order = round_bits(n)
    out = jnp.zeros_like(index)
    for place, b in enumerate(order):
        out = out | (((index >> place) & 1) << b)
    return out


def gather_rounds(piece, n):
    me = tensor_index()
    buf = piece[None]
    for b in round_bits(n):
        other = lax.ppermute(buf, TENSOR, [(i, i ^ (1 << b)) for i in range(n)])
        low = ((me >> b) & 1) == 0
        buf = jnp.concatenate(
            [jnp.where(low, buf, other), jnp.where(low, other, buf)], axis=0
        )
    return buf


def scatter_rounds(partial, n):
    bits = n.bit_length() - 1
    me = tensor_index()
    buf = partial.reshape((2,) * bits + partial.shape[1:])
    for b in reversed(round_bits(n)):
        mine = (me >> b) & 1
        keep = lax.dynamic_index_in_dim(buf, mine, 0, keepdims=False)
        send = lax.dynamic_index_in_dim(buf, 1 - mine, 0, keepdims=False)
        moved = lax.ppermute(
            send.astype(jnp.bfloat16), TENSOR, [(i, i ^ (1 << b)) for i in range(n)]
        )
        buf = keep + moved.astype(jnp.float32)
    return buf


def local(
    tokens,
    ln_gain,
    ln_bias,
    q_weight,
    kv_weight,
    dense_weight,
    up_weight,
    down_weight,
    kv_cache,
    cache_lengths,
):
    n = lax.axis_size("tx") * lax.axis_size("tz")
    bits = n.bit_length() - 1
    width = kv_weight.shape[1] // 2
    query_cols = q_weight.shape[1]
    heads_here = query_cols // width
    width_model = tokens.shape[-1]
    per_device = tokens.shape[1]

    mine = lax.all_to_all(kv_cache, "dp", split_axis=0, concat_axis=2, tiled=True)
    inner_all = mine.shape[2]
    gathered = lax.all_gather(mine, "tz", axis=1, tiled=True)
    gathered = lax.all_gather(gathered, "tx", axis=1, tiled=True)
    flat_keys = gathered[0].reshape(-1, 2 * width)

    normed = norm_rows(tokens[0], ln_gain, ln_bias)
    piece = gather_rounds(normed, n).reshape(n * per_device, width_model)
    projected = jnp.concatenate(
        [
            jnp.dot(piece, q_weight, preferred_element_type=jnp.float32),
            jnp.dot(piece, kv_weight, preferred_element_type=jnp.float32),
            jnp.dot(piece, up_weight, preferred_element_type=jnp.float32),
        ],
        axis=1,
    )
    span = projected.shape[0]
    row = jnp.arange(span, dtype=jnp.int32)
    token_pos = layout_source(row // per_device, n) * per_device + row % per_device
    group = lax.axis_index("dp")
    own_length = lax.dynamic_index_in_dim(cache_lengths, group, 0, keepdims=False)
    places = own_length + token_pos
    cosine, sine = rotary_tables(places, width)
    queries = rotate(
        projected[:, :query_cols].reshape(span, heads_here, width),
        cosine[:, None, :],
        sine[:, None, :],
    ).astype(jnp.bfloat16)
    new_keys = rotate(projected[:, query_cols : query_cols + width], cosine, sine).astype(
        jnp.bfloat16
    )
    new_values = projected[:, query_cols + width : query_cols + 2 * width].astype(jnp.bfloat16)
    hidden = jax.nn.gelu(projected[:, query_cols + 2 * width :], approximate=False).astype(
        jnp.bfloat16
    )
    rows = span * heads_here
    query_rows = queries.reshape(rows, width)
    places_piece = jnp.arange(flat_keys.shape[0], dtype=jnp.int32)
    valid = (places_piece < own_length)[None, :]
    state = lax.cond(
        jnp.int32(0) * inner_all < own_length,
        lambda carry: fold_keys(carry, query_rows, flat_keys, valid),
        lambda carry: carry,
        empty_state(rows, width, ()),
    )
    pos_of_row = jnp.repeat(token_pos, heads_here)
    causal = token_pos[None, :] <= pos_of_row[:, None]
    summed, best, total = absorb(state, query_rows, new_keys, new_values, causal)
    attn = (summed / total[:, None]).astype(jnp.bfloat16)
    partial = jnp.dot(attn, dense_weight, preferred_element_type=jnp.float32) + jnp.dot(
        hidden, down_weight, preferred_element_type=jnp.float32
    )
    layer_rows = scatter_rounds(partial.reshape(n, per_device, width_model), n)
    return (tokens[0].astype(jnp.float32) + layer_rows).astype(jnp.bfloat16)[None]


def solution(mesh):
    dp = mesh.shape["dp"]
    tensor = mesh.shape["tensor"]
    tx = 4 if tensor % 4 == 0 else 1
    mesh3 = Mesh(mesh.devices.reshape(dp, tx, tensor // tx), ("dp", "tx", "tz"))
    return jax.shard_map(
        local,
        mesh=mesh3,
        in_specs=(
            P("dp", TENSOR, None),
            P(),
            P(),
            P(None, TENSOR),
            P(),
            P(TENSOR, None),
            P(None, TENSOR),
            P(TENSOR, None),
            P(None, TENSOR, "dp", None),
            P(),
        ),
        out_specs=P("dp", TENSOR, None),
        check_vma=False,
    )
```

```python
import math

import jax
import jax.numpy as jnp
from jax import lax
from jax.sharding import Mesh
from jax.sharding import PartitionSpec as P

NEGATIVE = -1e30
TENSOR = ("tx", "tz")


def norm_rows(rows, gain, shift):
    widened = rows.astype(jnp.float32)
    center = jnp.mean(widened, axis=-1, keepdims=True)
    centered = widened - center
    variance = jnp.mean(centered * centered, axis=-1, keepdims=True)
    return (centered * lax.rsqrt(variance + 1e-05) * gain + shift).astype(jnp.bfloat16)


def rotary_tables(places, width):
    half = width // 2
    freqs = jnp.exp(jnp.arange(half, dtype=jnp.float32) * (-2.0 * math.log(10000.0) / width))
    angle = places.astype(jnp.float32)[..., None] * freqs
    cosine = jnp.concatenate([jnp.cos(angle), jnp.cos(angle)], axis=-1)
    sine = jnp.concatenate([jnp.sin(angle), jnp.sin(angle)], axis=-1)
    return (cosine, sine)


def rotate(values, cosine, sine):
    half = values.shape[-1] // 2
    turned = jnp.concatenate([-values[..., half:], values[..., :half]], axis=-1)
    return values * cosine + turned * sine


def combine(first, second):
    first_values, first_top, first_total = first
    second_values, second_top, second_total = second
    best = jnp.maximum(first_top, second_top)
    first_scale = jnp.exp(first_top - best)
    second_scale = jnp.exp(second_top - best)
    return (
        first_values * first_scale[..., None] + second_values * second_scale[..., None],
        best,
        first_total * first_scale + second_total * second_scale,
    )


def absorb(state, queries, key_rows, value_rows, valid):
    scores = jnp.dot(queries, key_rows.T, preferred_element_type=jnp.float32) * (
        1.0 / math.sqrt(queries.shape[-1])
    )
    scores = jnp.where(valid, scores, NEGATIVE)
    best = jnp.max(scores, axis=1)
    weights = jnp.exp(scores - best[:, None])
    block = (
        jnp.dot(weights.astype(jnp.bfloat16), value_rows, preferred_element_type=jnp.float32),
        best,
        jnp.sum(weights, axis=1),
    )
    return combine(state, block)


def fold_keys(state, queries, keys, valid):
    width = queries.shape[-1]
    return absorb(state, queries, keys[:, :width], keys[:, width:], valid)


def empty_state(rows, width, lead):
    return (
        jnp.zeros(lead + (rows, width), jnp.float32),
        jnp.full(lead + (rows,), NEGATIVE, jnp.float32),
        jnp.zeros(lead + (rows,), jnp.float32),
    )


def tensor_index():
    return lax.axis_index("tx") * lax.axis_size("tz") + lax.axis_index("tz")


def bit_reversed(index, bits):
    out = jnp.zeros_like(index)
    for b in range(bits):
        out = out | (((index >> b) & 1) << (bits - 1 - b))
    return out


def round_bits(n):
    bits = n.bit_length() - 1
    low = lax.axis_size("tz").bit_length() - 1
    return list(reversed(range(low))) + list(reversed(range(low, bits)))


def layout_source(index, n):
    order = round_bits(n)
    out = jnp.zeros_like(index)
    for place, b in enumerate(order):
        out = out | (((index >> place) & 1) << b)
    return out


def gather_rounds(piece, n):
    me = tensor_index()
    buf = piece[None]
    for b in round_bits(n):
        other = lax.ppermute(buf, TENSOR, [(i, i ^ (1 << b)) for i in range(n)])
        low = ((me >> b) & 1) == 0
        buf = jnp.concatenate(
            [jnp.where(low, buf, other), jnp.where(low, other, buf)], axis=0
        )
    return buf


def scatter_rounds(partial, n):
    bits = n.bit_length() - 1
    me = tensor_index()
    buf = partial.reshape((2,) * bits + partial.shape[1:])
    for b in reversed(round_bits(n)):
        mine = (me >> b) & 1
        keep = lax.dynamic_index_in_dim(buf, mine, 0, keepdims=False)
        send = lax.dynamic_index_in_dim(buf, 1 - mine, 0, keepdims=False)
        moved = lax.ppermute(
            send.astype(jnp.bfloat16), TENSOR, [(i, i ^ (1 << b)) for i in range(n)]
        )
        buf = keep + moved.astype(jnp.float32)
    return buf


def spread_from_first(x, name):
    size = lax.axis_size(name)
    me = lax.axis_index(name)
    have = 1
    while have < size:
        pairs = [(i, 2 * have - 1 - i) for i in range(have) if 2 * have - 1 - i < size]
        got = lax.ppermute(x, name, pairs)
        x = jnp.where((me >= have) & (me < 2 * have), got, x)
        have *= 2
    return x


def partial_state(queries, keys, values, valid):
    scores = jnp.einsum("...qd,...kd->...qk", queries, keys, preferred_element_type=jnp.float32)
    scores = scores * (1.0 / math.sqrt(queries.shape[-1]))
    scores = jnp.where(valid, scores, NEGATIVE)
    best = jnp.max(scores, axis=-1)
    weights = jnp.exp(scores - best[..., None])
    summed = jnp.einsum(
        "...qk,...kd->...qd",
        weights.astype(jnp.bfloat16),
        values,
        preferred_element_type=jnp.float32,
    )
    return (summed, best, jnp.sum(weights, axis=-1))


SHORT_MAX = 2048


def local(
    tokens,
    ln_gain,
    ln_bias,
    q_weight,
    kv_weight,
    dense_weight,
    up_weight,
    down_weight,
    kv_cache,
    cache_lengths,
):
    n = lax.axis_size("tx") * lax.axis_size("tz")
    width = kv_weight.shape[1] // 2
    query_cols = q_weight.shape[1]
    heads_here = query_cols // width
    width_model = tokens.shape[-1]
    per_device = tokens.shape[1]
    requests, blocks_here, inner_here = kv_cache.shape[:3]
    group = lax.axis_index("dp")
    inner_all = inner_here * lax.axis_size("dp")
    longest = jnp.argmax(cache_lengths).astype(jnp.int32)
    long_length = lax.dynamic_index_in_dim(cache_lengths, longest, 0, keepdims=False)
    inner_pos = group * inner_here + jnp.arange(inner_here, dtype=jnp.int32)

    long_local = lax.dynamic_index_in_dim(kv_cache, longest, 0, keepdims=False)
    long_all = gather_rounds(long_local, n)
    slot_src = layout_source(jnp.arange(n, dtype=jnp.int32), n)
    long_block = slot_src[:, None] * blocks_here + jnp.arange(blocks_here, dtype=jnp.int32)
    long_pos = (long_block[:, :, None] * inner_all + inner_pos).reshape(-1)
    long_keys = long_all.reshape(-1, 2 * width)

    short_blocks = -(-SHORT_MAX // inner_all)
    short_gath = lax.all_gather(kv_cache, "tz", axis=1, tiled=True)[:, :short_blocks]
    short_keys = spread_from_first(short_gath, "tx").reshape(requests, -1, 2 * width)
    short_pos = (jnp.arange(short_blocks, dtype=jnp.int32)[:, None] * inner_all + inner_pos).reshape(-1)

    normed = norm_rows(tokens[0], ln_gain, ln_bias)
    piece = gather_rounds(normed, n).reshape(n * per_device, width_model)
    projected = jnp.concatenate(
        [
            jnp.dot(piece, q_weight, preferred_element_type=jnp.float32),
            jnp.dot(piece, kv_weight, preferred_element_type=jnp.float32),
            jnp.dot(piece, up_weight, preferred_element_type=jnp.float32),
        ],
        axis=1,
    )
    span = projected.shape[0]
    row = jnp.arange(span, dtype=jnp.int32)
    token_pos = layout_source(row // per_device, n) * per_device + row % per_device
    own_length = lax.dynamic_index_in_dim(cache_lengths, group, 0, keepdims=False)
    places = own_length + token_pos
    cosine, sine = rotary_tables(places, width)
    queries = rotate(
        projected[:, :query_cols].reshape(span, heads_here, width),
        cosine[:, None, :],
        sine[:, None, :],
    ).astype(jnp.bfloat16)
    new_keys = rotate(projected[:, query_cols : query_cols + width], cosine, sine).astype(
        jnp.bfloat16
    )
    new_values = projected[:, query_cols + width : query_cols + 2 * width].astype(jnp.bfloat16)
    hidden = jax.nn.gelu(projected[:, query_cols + 2 * width :], approximate=False).astype(
        jnp.bfloat16
    )
    rows = span * heads_here
    query_rows = queries.reshape(rows, width)

    q_all = lax.all_gather(query_rows, "dp", axis=0, tiled=False)
    which = jnp.arange(requests, dtype=jnp.int32)
    short_valid = (short_pos[None, :] < cache_lengths[:, None]) & (which != longest)[:, None]
    short_state = partial_state(
        q_all, short_keys[..., :width], short_keys[..., width:], short_valid[:, None, :]
    )
    q_long = lax.dynamic_index_in_dim(q_all, longest, 0, keepdims=False)
    long_v, long_m, long_s = partial_state(
        q_long, long_keys[:, :width], long_keys[:, width:], (long_pos < long_length)[None, :]
    )
    is_long = which == longest
    state_all = combine(
        short_state,
        (
            jnp.where(is_long[:, None, None], long_v[None], 0.0),
            jnp.where(is_long[:, None], long_m[None], NEGATIVE),
            jnp.where(is_long[:, None], long_s[None], 0.0),
        ),
    )
    packed = jnp.concatenate(
        [state_all[0], state_all[1][..., None], state_all[2][..., None]], axis=-1
    )
    got = lax.all_to_all(packed, "dp", 0, 0, tiled=True)
    part_v, part_m, part_s = got[..., :width], got[..., width], got[..., width + 1]
    best = jnp.max(part_m, axis=0)
    scale = jnp.exp(part_m - best[None])
    state = (
        jnp.sum(part_v * scale[..., None], axis=0),
        best,
        jnp.sum(part_s * scale, axis=0),
    )

    pos_of_row = jnp.repeat(token_pos, heads_here)
    causal = token_pos[None, :] <= pos_of_row[:, None]
    summed, best, total = absorb(state, query_rows, new_keys, new_values, causal)
    attn = (summed / total[:, None]).astype(jnp.bfloat16)
    partial = jnp.dot(attn, dense_weight, preferred_element_type=jnp.float32) + jnp.dot(
        hidden, down_weight, preferred_element_type=jnp.float32
    )
    layer_rows = scatter_rounds(partial.reshape(n, per_device, width_model), n)
    return (tokens[0].astype(jnp.float32) + layer_rows).astype(jnp.bfloat16)[None]


def solution(mesh):
    dp = mesh.shape["dp"]
    tensor = mesh.shape["tensor"]
    tx = 4 if tensor % 4 == 0 else 1
    mesh3 = Mesh(mesh.devices.reshape(dp, tx, tensor // tx), ("dp", "tx", "tz"))
    return jax.shard_map(
        local,
        mesh=mesh3,
        in_specs=(
            P("dp", TENSOR, None),
            P(),
            P(),
            P(None, TENSOR),
            P(),
            P(TENSOR, None),
            P(None, TENSOR),
            P(TENSOR, None),
            P(None, TENSOR, "dp", None),
            P(),
        ),
        out_specs=P("dp", TENSOR, None),
        check_vma=False,
    )
```

```python
import math

import jax
import jax.numpy as jnp
from jax import lax
from jax.sharding import Mesh
from jax.sharding import PartitionSpec as P

NEGATIVE = -1e30
TENSOR = ("tx", "tz")


def norm_rows(rows, gain, shift):
    widened = rows.astype(jnp.float32)
    center = jnp.mean(widened, axis=-1, keepdims=True)
    centered = widened - center
    variance = jnp.mean(centered * centered, axis=-1, keepdims=True)
    return (centered * lax.rsqrt(variance + 1e-05) * gain + shift).astype(jnp.bfloat16)


def rotary_tables(places, width):
    half = width // 2
    freqs = jnp.exp(jnp.arange(half, dtype=jnp.float32) * (-2.0 * math.log(10000.0) / width))
    angle = places.astype(jnp.float32)[..., None] * freqs
    cosine = jnp.concatenate([jnp.cos(angle), jnp.cos(angle)], axis=-1)
    sine = jnp.concatenate([jnp.sin(angle), jnp.sin(angle)], axis=-1)
    return (cosine, sine)


def rotate(values, cosine, sine):
    half = values.shape[-1] // 2
    turned = jnp.concatenate([-values[..., half:], values[..., :half]], axis=-1)
    return values * cosine + turned * sine


def combine(first, second):
    first_values, first_top, first_total = first
    second_values, second_top, second_total = second
    best = jnp.maximum(first_top, second_top)
    first_scale = jnp.exp(first_top - best)
    second_scale = jnp.exp(second_top - best)
    return (
        first_values * first_scale[..., None] + second_values * second_scale[..., None],
        best,
        first_total * first_scale + second_total * second_scale,
    )


def absorb(state, queries, key_rows, value_rows, valid):
    scores = jnp.dot(queries, key_rows.T, preferred_element_type=jnp.float32) * (
        1.0 / math.sqrt(queries.shape[-1])
    )
    scores = jnp.where(valid, scores, NEGATIVE)
    best = jnp.max(scores, axis=1)
    weights = jnp.exp(scores - best[:, None])
    block = (
        jnp.dot(weights.astype(jnp.bfloat16), value_rows, preferred_element_type=jnp.float32),
        best,
        jnp.sum(weights, axis=1),
    )
    return combine(state, block)


def fold_keys(state, queries, keys, valid):
    width = queries.shape[-1]
    return absorb(state, queries, keys[:, :width], keys[:, width:], valid)


def empty_state(rows, width, lead):
    return (
        jnp.zeros(lead + (rows, width), jnp.float32),
        jnp.full(lead + (rows,), NEGATIVE, jnp.float32),
        jnp.zeros(lead + (rows,), jnp.float32),
    )


def tensor_index():
    return lax.axis_index("tx") * lax.axis_size("tz") + lax.axis_index("tz")


def bit_reversed(index, bits):
    out = jnp.zeros_like(index)
    for b in range(bits):
        out = out | (((index >> b) & 1) << (bits - 1 - b))
    return out


def round_bits(n):
    bits = n.bit_length() - 1
    low = lax.axis_size("tz").bit_length() - 1
    return list(reversed(range(low))) + list(reversed(range(low, bits)))


def layout_source(index, n):
    order = round_bits(n)
    out = jnp.zeros_like(index)
    for place, b in enumerate(order):
        out = out | (((index >> place) & 1) << b)
    return out


def gather_rounds(piece, n):
    me = tensor_index()
    buf = piece[None]
    for b in round_bits(n):
        other = lax.ppermute(buf, TENSOR, [(i, i ^ (1 << b)) for i in range(n)])
        low = ((me >> b) & 1) == 0
        buf = jnp.concatenate(
            [jnp.where(low, buf, other), jnp.where(low, other, buf)], axis=0
        )
    return buf


def scatter_rounds(partial, n):
    bits = n.bit_length() - 1
    me = tensor_index()
    buf = partial.reshape((2,) * bits + partial.shape[1:])
    for b in reversed(round_bits(n)):
        mine = (me >> b) & 1
        keep = lax.dynamic_index_in_dim(buf, mine, 0, keepdims=False)
        send = lax.dynamic_index_in_dim(buf, 1 - mine, 0, keepdims=False)
        moved = lax.ppermute(
            send.astype(jnp.bfloat16), TENSOR, [(i, i ^ (1 << b)) for i in range(n)]
        )
        buf = keep + moved.astype(jnp.float32)
    return buf


def spread_from_first(x, name):
    size = lax.axis_size(name)
    me = lax.axis_index(name)
    have = 1
    while have < size:
        pairs = [(i, 2 * have - 1 - i) for i in range(have) if 2 * have - 1 - i < size]
        got = lax.ppermute(x, name, pairs)
        x = jnp.where((me >= have) & (me < 2 * have), got, x)
        have *= 2
    return x


def partial_state(queries, keys, values, valid):
    scores = jnp.einsum("...qd,...kd->...qk", queries, keys, preferred_element_type=jnp.float32)
    scores = scores * (1.0 / math.sqrt(queries.shape[-1]))
    scores = jnp.where(valid, scores, NEGATIVE)
    best = jnp.max(scores, axis=-1)
    weights = jnp.exp(scores - best[..., None])
    summed = jnp.einsum(
        "...qk,...kd->...qd",
        weights.astype(jnp.bfloat16),
        values,
        preferred_element_type=jnp.float32,
    )
    return (summed, best, jnp.sum(weights, axis=-1))


SHORT_MAX = 2048


def z_rounds(piece):
    size = lax.axis_size("tz")
    me = lax.axis_index("tz")
    buf = piece[None]
    for b in reversed(range(size.bit_length() - 1)):
        other = lax.ppermute(buf, "tz", [(i, i ^ (1 << b)) for i in range(size)])
        low = ((me >> b) & 1) == 0
        buf = jnp.concatenate(
            [jnp.where(low, buf, other), jnp.where(low, other, buf)], axis=0
        )
    return buf


def gather_tensor(piece):
    nx = lax.axis_size("tx")
    buf = z_rounds(piece)
    wide = jnp.broadcast_to(buf[None], (nx,) + buf.shape)
    return lax.all_to_all(wide, "tx", 0, 0, tiled=True).reshape((-1,) + piece.shape)


def slot_source(index):
    nz = lax.axis_size("tz")
    return (index // nz) * nz + bit_reversed(index % nz, nz.bit_length() - 1)


def scatter_tensor(partial):
    nx, nz = lax.axis_size("tx"), lax.axis_size("tz")
    bits = nz.bit_length() - 1
    buf = partial.reshape((nx, nz) + partial.shape[1:]).astype(jnp.bfloat16)
    over_x = lax.all_to_all(buf, "tx", 0, 0, tiled=True).astype(jnp.float32).sum(0)
    order = [int(format(c, f"0{bits}b")[::-1], 2) if bits else 0 for c in range(nz)]
    ready = jnp.take(over_x, jnp.array(order, dtype=jnp.int32), axis=0).astype(jnp.bfloat16)
    return lax.all_to_all(ready, "tz", 0, 0, tiled=True).astype(jnp.float32).sum(0)


def local(
    tokens,
    ln_gain,
    ln_bias,
    q_weight,
    kv_weight,
    dense_weight,
    up_weight,
    down_weight,
    kv_cache,
    cache_lengths,
):
    n = lax.axis_size("tx") * lax.axis_size("tz")
    width = kv_weight.shape[1] // 2
    query_cols = q_weight.shape[1]
    heads_here = query_cols // width
    width_model = tokens.shape[-1]
    per_device = tokens.shape[1]
    requests, blocks_here, inner_here = kv_cache.shape[:3]
    group = lax.axis_index("dp")
    inner_all = inner_here * lax.axis_size("dp")
    longest = jnp.argmax(cache_lengths).astype(jnp.int32)
    long_length = lax.dynamic_index_in_dim(cache_lengths, longest, 0, keepdims=False)
    inner_pos = group * inner_here + jnp.arange(inner_here, dtype=jnp.int32)

    long_local = lax.dynamic_index_in_dim(kv_cache, longest, 0, keepdims=False)
    normed = norm_rows(tokens[0], ln_gain, ln_bias)
    both = gather_tensor(jnp.concatenate([normed.reshape(-1), long_local.reshape(-1)]))
    token_cut = normed.size
    long_all = both[:, token_cut:].reshape((n,) + long_local.shape)
    slot_src = slot_source(jnp.arange(n, dtype=jnp.int32))
    long_block = slot_src[:, None] * blocks_here + jnp.arange(blocks_here, dtype=jnp.int32)
    long_pos = (long_block[:, :, None] * inner_all + inner_pos).reshape(-1)
    long_keys = long_all.reshape(-1, 2 * width)

    short_blocks = -(-SHORT_MAX // inner_all)
    short_gath = lax.all_gather(kv_cache, "tz", axis=1, tiled=True)[:, :short_blocks]
    short_keys = spread_from_first(short_gath, "tx").reshape(requests, -1, 2 * width)
    short_pos = (jnp.arange(short_blocks, dtype=jnp.int32)[:, None] * inner_all + inner_pos).reshape(-1)

    piece = both[:, :token_cut].reshape(n * per_device, width_model)
    projected = jnp.concatenate(
        [
            jnp.dot(piece, q_weight, preferred_element_type=jnp.float32),
            jnp.dot(piece, kv_weight, preferred_element_type=jnp.float32),
            jnp.dot(piece, up_weight, preferred_element_type=jnp.float32),
        ],
        axis=1,
    )
    span = projected.shape[0]
    row = jnp.arange(span, dtype=jnp.int32)
    token_pos = slot_source(row // per_device) * per_device + row % per_device
    own_length = lax.dynamic_index_in_dim(cache_lengths, group, 0, keepdims=False)
    places = own_length + token_pos
    cosine, sine = rotary_tables(places, width)
    queries = rotate(
        projected[:, :query_cols].reshape(span, heads_here, width),
        cosine[:, None, :],
        sine[:, None, :],
    ).astype(jnp.bfloat16)
    new_keys = rotate(projected[:, query_cols : query_cols + width], cosine, sine).astype(
        jnp.bfloat16
    )
    new_values = projected[:, query_cols + width : query_cols + 2 * width].astype(jnp.bfloat16)
    hidden = jax.nn.gelu(projected[:, query_cols + 2 * width :], approximate=False).astype(
        jnp.bfloat16
    )
    rows = span * heads_here
    query_rows = queries.reshape(rows, width)

    q_all = lax.all_gather(query_rows, "dp", axis=0, tiled=False)
    which = jnp.arange(requests, dtype=jnp.int32)
    short_valid = (short_pos[None, :] < cache_lengths[:, None]) & (which != longest)[:, None]
    short_state = partial_state(
        q_all, short_keys[..., :width], short_keys[..., width:], short_valid[:, None, :]
    )
    q_long = lax.dynamic_index_in_dim(q_all, longest, 0, keepdims=False)
    long_v, long_m, long_s = partial_state(
        q_long, long_keys[:, :width], long_keys[:, width:], (long_pos < long_length)[None, :]
    )
    is_long = which == longest
    state_all = combine(
        short_state,
        (
            jnp.where(is_long[:, None, None], long_v[None], 0.0),
            jnp.where(is_long[:, None], long_m[None], NEGATIVE),
            jnp.where(is_long[:, None], long_s[None], 0.0),
        ),
    )
    packed = jnp.concatenate(
        [state_all[0], state_all[1][..., None], state_all[2][..., None]], axis=-1
    )
    got = lax.all_to_all(packed, "dp", 0, 0, tiled=True)
    part_v, part_m, part_s = got[..., :width], got[..., width], got[..., width + 1]
    best = jnp.max(part_m, axis=0)
    scale = jnp.exp(part_m - best[None])
    state = (
        jnp.sum(part_v * scale[..., None], axis=0),
        best,
        jnp.sum(part_s * scale, axis=0),
    )

    pos_of_row = jnp.repeat(token_pos, heads_here)
    causal = token_pos[None, :] <= pos_of_row[:, None]
    summed, best, total = absorb(state, query_rows, new_keys, new_values, causal)
    attn = (summed / total[:, None]).astype(jnp.bfloat16)
    partial = jnp.dot(attn, dense_weight, preferred_element_type=jnp.float32) + jnp.dot(
        hidden, down_weight, preferred_element_type=jnp.float32
    )
    layer_rows = scatter_tensor(partial.reshape(n, per_device, width_model))
    return (tokens[0].astype(jnp.float32) + layer_rows).astype(jnp.bfloat16)[None]


def solution(mesh):
    dp = mesh.shape["dp"]
    tensor = mesh.shape["tensor"]
    tx = 4 if tensor % 4 == 0 else 1
    mesh3 = Mesh(mesh.devices.reshape(dp, tx, tensor // tx), ("dp", "tx", "tz"))
    return jax.shard_map(
        local,
        mesh=mesh3,
        in_specs=(
            P("dp", TENSOR, None),
            P(),
            P(),
            P(None, TENSOR),
            P(),
            P(TENSOR, None),
            P(None, TENSOR),
            P(TENSOR, None),
            P(None, TENSOR, "dp", None),
            P(),
        ),
        out_specs=P("dp", TENSOR, None),
        check_vma=False,
    )
```

```python
import math

import jax
import jax.numpy as jnp
from jax import lax
from jax.sharding import Mesh
from jax.sharding import PartitionSpec as P

NEGATIVE = -1e30
TENSOR = ("tx", "tz")


def norm_rows(rows, gain, shift):
    widened = rows.astype(jnp.float32)
    center = jnp.mean(widened, axis=-1, keepdims=True)
    centered = widened - center
    variance = jnp.mean(centered * centered, axis=-1, keepdims=True)
    return (centered * lax.rsqrt(variance + 1e-05) * gain + shift).astype(jnp.bfloat16)


def rotary_tables(places, width):
    half = width // 2
    freqs = jnp.exp(jnp.arange(half, dtype=jnp.float32) * (-2.0 * math.log(10000.0) / width))
    angle = places.astype(jnp.float32)[..., None] * freqs
    cosine = jnp.concatenate([jnp.cos(angle), jnp.cos(angle)], axis=-1)
    sine = jnp.concatenate([jnp.sin(angle), jnp.sin(angle)], axis=-1)
    return (cosine, sine)


def rotate(values, cosine, sine):
    half = values.shape[-1] // 2
    turned = jnp.concatenate([-values[..., half:], values[..., :half]], axis=-1)
    return values * cosine + turned * sine


def combine(first, second):
    first_values, first_top, first_total = first
    second_values, second_top, second_total = second
    best = jnp.maximum(first_top, second_top)
    first_scale = jnp.exp(first_top - best)
    second_scale = jnp.exp(second_top - best)
    return (
        first_values * first_scale[..., None] + second_values * second_scale[..., None],
        best,
        first_total * first_scale + second_total * second_scale,
    )


def absorb(state, queries, key_rows, value_rows, valid):
    scores = jnp.dot(queries, key_rows.T, preferred_element_type=jnp.float32) * (
        1.0 / math.sqrt(queries.shape[-1])
    )
    scores = jnp.where(valid, scores, NEGATIVE)
    best = jnp.max(scores, axis=1)
    weights = jnp.exp(scores - best[:, None])
    block = (
        jnp.dot(weights.astype(jnp.bfloat16), value_rows, preferred_element_type=jnp.float32),
        best,
        jnp.sum(weights, axis=1),
    )
    return combine(state, block)


def fold_keys(state, queries, keys, valid):
    width = queries.shape[-1]
    return absorb(state, queries, keys[:, :width], keys[:, width:], valid)


def empty_state(rows, width, lead):
    return (
        jnp.zeros(lead + (rows, width), jnp.float32),
        jnp.full(lead + (rows,), NEGATIVE, jnp.float32),
        jnp.zeros(lead + (rows,), jnp.float32),
    )


def tensor_index():
    return lax.axis_index("tx") * lax.axis_size("tz") + lax.axis_index("tz")


def bit_reversed(index, bits):
    out = jnp.zeros_like(index)
    for b in range(bits):
        out = out | (((index >> b) & 1) << (bits - 1 - b))
    return out


def round_bits(n):
    bits = n.bit_length() - 1
    low = lax.axis_size("tz").bit_length() - 1
    return list(reversed(range(low))) + list(reversed(range(low, bits)))


def layout_source(index, n):
    order = round_bits(n)
    out = jnp.zeros_like(index)
    for place, b in enumerate(order):
        out = out | (((index >> place) & 1) << b)
    return out


def gather_rounds(piece, n):
    me = tensor_index()
    buf = piece[None]
    for b in round_bits(n):
        other = lax.ppermute(buf, TENSOR, [(i, i ^ (1 << b)) for i in range(n)])
        low = ((me >> b) & 1) == 0
        buf = jnp.concatenate(
            [jnp.where(low, buf, other), jnp.where(low, other, buf)], axis=0
        )
    return buf


def scatter_rounds(partial, n):
    bits = n.bit_length() - 1
    me = tensor_index()
    buf = partial.reshape((2,) * bits + partial.shape[1:])
    for b in reversed(round_bits(n)):
        mine = (me >> b) & 1
        keep = lax.dynamic_index_in_dim(buf, mine, 0, keepdims=False)
        send = lax.dynamic_index_in_dim(buf, 1 - mine, 0, keepdims=False)
        moved = lax.ppermute(
            send.astype(jnp.bfloat16), TENSOR, [(i, i ^ (1 << b)) for i in range(n)]
        )
        buf = keep + moved.astype(jnp.float32)
    return buf


def spread_from_first(x, name):
    size = lax.axis_size(name)
    me = lax.axis_index(name)
    have = 1
    while have < size:
        pairs = [(i, 2 * have - 1 - i) for i in range(have) if 2 * have - 1 - i < size]
        got = lax.ppermute(x, name, pairs)
        x = jnp.where((me >= have) & (me < 2 * have), got, x)
        have *= 2
    return x


def partial_state(queries, keys, values, valid):
    scores = jnp.einsum("...qd,...kd->...qk", queries, keys, preferred_element_type=jnp.float32)
    scores = scores * (1.0 / math.sqrt(queries.shape[-1]))
    scores = jnp.where(valid, scores, NEGATIVE)
    best = jnp.max(scores, axis=-1)
    weights = jnp.exp(scores - best[..., None])
    summed = jnp.einsum(
        "...qk,...kd->...qd",
        weights.astype(jnp.bfloat16),
        values,
        preferred_element_type=jnp.float32,
    )
    return (summed, best, jnp.sum(weights, axis=-1))


SHORT_MAX = 2048


def z_rounds(piece):
    size = lax.axis_size("tz")
    me = lax.axis_index("tz")
    buf = piece[None]
    for b in reversed(range(size.bit_length() - 1)):
        other = lax.ppermute(buf, "tz", [(i, i ^ (1 << b)) for i in range(size)])
        low = ((me >> b) & 1) == 0
        buf = jnp.concatenate(
            [jnp.where(low, buf, other), jnp.where(low, other, buf)], axis=0
        )
    return buf


def gather_tensor(piece):
    nx = lax.axis_size("tx")
    buf = z_rounds(piece)
    wide = jnp.broadcast_to(buf[None], (nx,) + buf.shape)
    return lax.all_to_all(wide, "tx", 0, 0, tiled=True).reshape((-1,) + piece.shape)


def slot_source(index):
    nz = lax.axis_size("tz")
    return (index // nz) * nz + bit_reversed(index % nz, nz.bit_length() - 1)


def scatter_tensor(partial):
    nx, nz = lax.axis_size("tx"), lax.axis_size("tz")
    bits = nz.bit_length() - 1
    buf = partial.reshape((nx, nz) + partial.shape[1:]).astype(jnp.bfloat16)
    over_x = lax.all_to_all(buf, "tx", 0, 0, tiled=True).astype(jnp.float32).sum(0)
    order = [int(format(c, f"0{bits}b")[::-1], 2) if bits else 0 for c in range(nz)]
    ready = jnp.take(over_x, jnp.array(order, dtype=jnp.int32), axis=0).astype(jnp.bfloat16)
    return lax.all_to_all(ready, "tz", 0, 0, tiled=True).astype(jnp.float32).sum(0)


def local(
    tokens,
    ln_gain,
    ln_bias,
    q_weight,
    kv_weight,
    dense_weight,
    up_weight,
    down_weight,
    kv_cache,
    cache_lengths,
):
    n = lax.axis_size("tx") * lax.axis_size("tz")
    width = kv_weight.shape[1] // 2
    query_cols = q_weight.shape[1]
    heads_here = query_cols // width
    width_model = tokens.shape[-1]
    per_device = tokens.shape[1]
    requests, blocks_here, inner_here = kv_cache.shape[:3]
    group = lax.axis_index("dp")
    inner_all = inner_here * lax.axis_size("dp")
    longest = jnp.argmax(cache_lengths).astype(jnp.int32)
    long_length = lax.dynamic_index_in_dim(cache_lengths, longest, 0, keepdims=False)
    inner_pos = group * inner_here + jnp.arange(inner_here, dtype=jnp.int32)

    long_local = lax.dynamic_index_in_dim(kv_cache, longest, 0, keepdims=False)
    normed = norm_rows(tokens[0], ln_gain, ln_bias)
    both = gather_tensor(jnp.concatenate([normed.reshape(-1), long_local.reshape(-1)]))
    token_cut = normed.size
    long_all = both[:, token_cut:].reshape((n,) + long_local.shape)
    slot_src = slot_source(jnp.arange(n, dtype=jnp.int32))
    long_block = slot_src[:, None] * blocks_here + jnp.arange(blocks_here, dtype=jnp.int32)
    long_pos = (long_block[:, :, None] * inner_all + inner_pos).reshape(-1)
    long_keys = long_all.reshape(-1, 2 * width)

    short_blocks = -(-SHORT_MAX // inner_all)
    short_gath = lax.all_gather(kv_cache, "tz", axis=1, tiled=True)[:, :short_blocks]
    short_pos = (jnp.arange(short_blocks, dtype=jnp.int32)[:, None] * inner_all + inner_pos).reshape(-1)

    piece = both[:, :token_cut].reshape(n * per_device, width_model)
    projected = jnp.concatenate(
        [
            jnp.dot(piece, q_weight, preferred_element_type=jnp.float32),
            jnp.dot(piece, kv_weight, preferred_element_type=jnp.float32),
            jnp.dot(piece, up_weight, preferred_element_type=jnp.float32),
        ],
        axis=1,
    )
    span = projected.shape[0]
    row = jnp.arange(span, dtype=jnp.int32)
    token_pos = slot_source(row // per_device) * per_device + row % per_device
    own_length = lax.dynamic_index_in_dim(cache_lengths, group, 0, keepdims=False)
    places = own_length + token_pos
    cosine, sine = rotary_tables(places, width)
    queries = rotate(
        projected[:, :query_cols].reshape(span, heads_here, width),
        cosine[:, None, :],
        sine[:, None, :],
    ).astype(jnp.bfloat16)
    new_keys = rotate(projected[:, query_cols : query_cols + width], cosine, sine).astype(
        jnp.bfloat16
    )
    new_values = projected[:, query_cols + width : query_cols + 2 * width].astype(jnp.bfloat16)
    hidden = jax.nn.gelu(projected[:, query_cols + 2 * width :], approximate=False).astype(
        jnp.bfloat16
    )
    rows = span * heads_here
    query_rows = queries.reshape(rows, width)

    q_all = lax.all_gather(query_rows, "dp", axis=0, tiled=False)
    q_long = lax.dynamic_index_in_dim(q_all, longest, 0, keepdims=False)
    long_v, long_m, long_s = partial_state(
        q_long, long_keys[:, :width], long_keys[:, width:], (long_pos < long_length)[None, :]
    )
    down_part = jnp.dot(hidden, down_weight, preferred_element_type=jnp.float32)
    short_gath, long_v, long_m, long_s, down_part = lax.optimization_barrier(
        (short_gath, long_v, long_m, long_s, down_part)
    )
    short_keys = spread_from_first(short_gath, "tx").reshape(requests, -1, 2 * width)
    which = jnp.arange(requests, dtype=jnp.int32)
    short_valid = (short_pos[None, :] < cache_lengths[:, None]) & (which != longest)[:, None]
    short_state = partial_state(
        q_all, short_keys[..., :width], short_keys[..., width:], short_valid[:, None, :]
    )
    is_long = which == longest
    state_all = combine(
        short_state,
        (
            jnp.where(is_long[:, None, None], long_v[None], 0.0),
            jnp.where(is_long[:, None], long_m[None], NEGATIVE),
            jnp.where(is_long[:, None], long_s[None], 0.0),
        ),
    )
    packed = jnp.concatenate(
        [state_all[0], state_all[1][..., None], state_all[2][..., None]], axis=-1
    )
    got = lax.all_to_all(packed, "dp", 0, 0, tiled=True)
    part_v, part_m, part_s = got[..., :width], got[..., width], got[..., width + 1]
    best = jnp.max(part_m, axis=0)
    scale = jnp.exp(part_m - best[None])
    state = (
        jnp.sum(part_v * scale[..., None], axis=0),
        best,
        jnp.sum(part_s * scale, axis=0),
    )

    pos_of_row = jnp.repeat(token_pos, heads_here)
    causal = token_pos[None, :] <= pos_of_row[:, None]
    summed, best, total = absorb(state, query_rows, new_keys, new_values, causal)
    attn = (summed / total[:, None]).astype(jnp.bfloat16)
    partial = jnp.dot(attn, dense_weight, preferred_element_type=jnp.float32) + down_part
    layer_rows = scatter_tensor(partial.reshape(n, per_device, width_model))
    return (tokens[0].astype(jnp.float32) + layer_rows).astype(jnp.bfloat16)[None]


def solution(mesh):
    dp = mesh.shape["dp"]
    tensor = mesh.shape["tensor"]
    tx = 4 if tensor % 4 == 0 else 1
    mesh3 = Mesh(mesh.devices.reshape(dp, tx, tensor // tx), ("dp", "tx", "tz"))
    return jax.shard_map(
        local,
        mesh=mesh3,
        in_specs=(
            P("dp", TENSOR, None),
            P(),
            P(),
            P(None, TENSOR),
            P(),
            P(TENSOR, None),
            P(None, TENSOR),
            P(TENSOR, None),
            P(None, TENSOR, "dp", None),
            P(),
        ),
        out_specs=P("dp", TENSOR, None),
        check_vma=False,
    )
```

```python
import math

import jax
import jax.numpy as jnp
from jax import lax
from jax.sharding import Mesh
from jax.sharding import PartitionSpec as P

NEGATIVE = -1e30
TENSOR = ("tx", "tz")


def norm_rows(rows, gain, shift):
    widened = rows.astype(jnp.float32)
    center = jnp.mean(widened, axis=-1, keepdims=True)
    centered = widened - center
    variance = jnp.mean(centered * centered, axis=-1, keepdims=True)
    return (centered * lax.rsqrt(variance + 1e-05) * gain + shift).astype(jnp.bfloat16)


def rotary_tables(places, width):
    half = width // 2
    freqs = jnp.exp(jnp.arange(half, dtype=jnp.float32) * (-2.0 * math.log(10000.0) / width))
    angle = places.astype(jnp.float32)[..., None] * freqs
    cosine = jnp.concatenate([jnp.cos(angle), jnp.cos(angle)], axis=-1)
    sine = jnp.concatenate([jnp.sin(angle), jnp.sin(angle)], axis=-1)
    return (cosine, sine)


def rotate(values, cosine, sine):
    half = values.shape[-1] // 2
    turned = jnp.concatenate([-values[..., half:], values[..., :half]], axis=-1)
    return values * cosine + turned * sine


def combine(first, second):
    first_values, first_top, first_total = first
    second_values, second_top, second_total = second
    best = jnp.maximum(first_top, second_top)
    first_scale = jnp.exp(first_top - best)
    second_scale = jnp.exp(second_top - best)
    return (
        first_values * first_scale[..., None] + second_values * second_scale[..., None],
        best,
        first_total * first_scale + second_total * second_scale,
    )


def absorb(state, queries, key_rows, value_rows, valid):
    scores = jnp.dot(queries, key_rows.T, preferred_element_type=jnp.float32) * (
        1.0 / math.sqrt(queries.shape[-1])
    )
    scores = jnp.where(valid, scores, NEGATIVE)
    best = jnp.max(scores, axis=1)
    weights = jnp.exp(scores - best[:, None])
    block = (
        jnp.dot(weights.astype(jnp.bfloat16), value_rows, preferred_element_type=jnp.float32),
        best,
        jnp.sum(weights, axis=1),
    )
    return combine(state, block)


def fold_keys(state, queries, keys, valid):
    width = queries.shape[-1]
    return absorb(state, queries, keys[:, :width], keys[:, width:], valid)


def empty_state(rows, width, lead):
    return (
        jnp.zeros(lead + (rows, width), jnp.float32),
        jnp.full(lead + (rows,), NEGATIVE, jnp.float32),
        jnp.zeros(lead + (rows,), jnp.float32),
    )


def tensor_index():
    return lax.axis_index("tx") * lax.axis_size("tz") + lax.axis_index("tz")


def bit_reversed(index, bits):
    out = jnp.zeros_like(index)
    for b in range(bits):
        out = out | (((index >> b) & 1) << (bits - 1 - b))
    return out


def round_bits(n):
    bits = n.bit_length() - 1
    low = lax.axis_size("tz").bit_length() - 1
    return list(reversed(range(low))) + list(reversed(range(low, bits)))


def layout_source(index, n):
    order = round_bits(n)
    out = jnp.zeros_like(index)
    for place, b in enumerate(order):
        out = out | (((index >> place) & 1) << b)
    return out


def gather_rounds(piece, n):
    me = tensor_index()
    buf = piece[None]
    for b in round_bits(n):
        other = lax.ppermute(buf, TENSOR, [(i, i ^ (1 << b)) for i in range(n)])
        low = ((me >> b) & 1) == 0
        buf = jnp.concatenate(
            [jnp.where(low, buf, other), jnp.where(low, other, buf)], axis=0
        )
    return buf


def scatter_rounds(partial, n):
    bits = n.bit_length() - 1
    me = tensor_index()
    buf = partial.reshape((2,) * bits + partial.shape[1:])
    for b in reversed(round_bits(n)):
        mine = (me >> b) & 1
        keep = lax.dynamic_index_in_dim(buf, mine, 0, keepdims=False)
        send = lax.dynamic_index_in_dim(buf, 1 - mine, 0, keepdims=False)
        moved = lax.ppermute(
            send.astype(jnp.bfloat16), TENSOR, [(i, i ^ (1 << b)) for i in range(n)]
        )
        buf = keep + moved.astype(jnp.float32)
    return buf


def spread_from_first(x, name):
    size = lax.axis_size(name)
    me = lax.axis_index(name)
    have = 1
    while have < size:
        pairs = [(i, 2 * have - 1 - i) for i in range(have) if 2 * have - 1 - i < size]
        got = lax.ppermute(x, name, pairs)
        x = jnp.where((me >= have) & (me < 2 * have), got, x)
        have *= 2
    return x


def partial_state(queries, keys, values, valid):
    scores = jnp.einsum("...qd,...kd->...qk", queries, keys, preferred_element_type=jnp.float32)
    scores = scores * (1.0 / math.sqrt(queries.shape[-1]))
    scores = jnp.where(valid, scores, NEGATIVE)
    best = jnp.max(scores, axis=-1)
    weights = jnp.exp(scores - best[..., None])
    summed = jnp.einsum(
        "...qk,...kd->...qd",
        weights.astype(jnp.bfloat16),
        values,
        preferred_element_type=jnp.float32,
    )
    return (summed, best, jnp.sum(weights, axis=-1))


SHORT_MAX = 2048


def z_groups(size):
    groups, b = [], size.bit_length() - 1
    while b > 0:
        lo = max(b - 2, 0)
        groups.append((lo, b - lo))
        b = lo
    return groups


def z_source(slot, size):
    out, offset = 0, 0
    for lo, width in z_groups(size):
        out |= ((slot >> offset) & ((1 << width) - 1)) << lo
        offset += width
    return out


def z_rounds(piece):
    size = lax.axis_size("tz")
    me = lax.axis_index("tz")
    buf = piece[None]
    for lo, width in z_groups(size):
        radix = 1 << width
        mine = (me >> lo) & (radix - 1)
        got = [buf] + [
            lax.ppermute(buf, "tz", [(i, i ^ (k << lo)) for i in range(size)])
            for k in range(1, radix)
        ]
        stacked = jnp.stack(got)
        buf = jnp.stack(
            [lax.dynamic_index_in_dim(stacked, v ^ mine, 0, keepdims=False) for v in range(radix)]
        ).reshape((-1,) + piece.shape)
    return buf


def gather_tensor(piece):
    nx = lax.axis_size("tx")
    buf = z_rounds(piece)
    wide = jnp.broadcast_to(buf[None], (nx,) + buf.shape)
    return lax.all_to_all(wide, "tx", 0, 0, tiled=True).reshape((-1,) + piece.shape)


def slot_source(index):
    nz = lax.axis_size("tz")
    table = jnp.array([z_source(s, nz) for s in range(nz)], dtype=jnp.int32)
    return (index // nz) * nz + table[index % nz]


def scatter_tensor(partial):
    nx, nz = lax.axis_size("tx"), lax.axis_size("tz")
    bits = nz.bit_length() - 1
    buf = partial.reshape((nx, nz) + partial.shape[1:]).astype(jnp.bfloat16)
    over_x = lax.all_to_all(buf, "tx", 0, 0, tiled=True).astype(jnp.float32).sum(0)
    order = [next(s for s in range(nz) if z_source(s, nz) == c) for c in range(nz)]
    ready = jnp.take(over_x, jnp.array(order, dtype=jnp.int32), axis=0).astype(jnp.bfloat16)
    return lax.all_to_all(ready, "tz", 0, 0, tiled=True).astype(jnp.float32).sum(0)


def local(
    tokens,
    ln_gain,
    ln_bias,
    q_weight,
    kv_weight,
    dense_weight,
    up_weight,
    down_weight,
    kv_cache,
    cache_lengths,
):
    n = lax.axis_size("tx") * lax.axis_size("tz")
    width = kv_weight.shape[1] // 2
    query_cols = q_weight.shape[1]
    heads_here = query_cols // width
    width_model = tokens.shape[-1]
    per_device = tokens.shape[1]
    requests, blocks_here, inner_here = kv_cache.shape[:3]
    group = lax.axis_index("dp")
    inner_all = inner_here * lax.axis_size("dp")
    longest = jnp.argmax(cache_lengths).astype(jnp.int32)
    long_length = lax.dynamic_index_in_dim(cache_lengths, longest, 0, keepdims=False)
    inner_pos = group * inner_here + jnp.arange(inner_here, dtype=jnp.int32)

    long_local = lax.dynamic_index_in_dim(kv_cache, longest, 0, keepdims=False)
    normed = norm_rows(tokens[0], ln_gain, ln_bias)
    both = gather_tensor(jnp.concatenate([normed.reshape(-1), long_local.reshape(-1)]))
    token_cut = normed.size
    long_all = both[:, token_cut:].reshape((n,) + long_local.shape)
    slot_src = slot_source(jnp.arange(n, dtype=jnp.int32))
    long_block = slot_src[:, None] * blocks_here + jnp.arange(blocks_here, dtype=jnp.int32)
    long_pos = (long_block[:, :, None] * inner_all + inner_pos).reshape(-1)
    long_keys = long_all.reshape(-1, 2 * width)

    short_blocks = -(-SHORT_MAX // inner_all)
    short_gath = lax.all_gather(kv_cache, "tz", axis=1, tiled=True)[:, :short_blocks]
    short_pos = (jnp.arange(short_blocks, dtype=jnp.int32)[:, None] * inner_all + inner_pos).reshape(-1)

    piece = both[:, :token_cut].reshape(n * per_device, width_model)
    projected = jnp.concatenate(
        [
            jnp.dot(piece, q_weight, preferred_element_type=jnp.float32),
            jnp.dot(piece, kv_weight, preferred_element_type=jnp.float32),
            jnp.dot(piece, up_weight, preferred_element_type=jnp.float32),
        ],
        axis=1,
    )
    span = projected.shape[0]
    row = jnp.arange(span, dtype=jnp.int32)
    token_pos = slot_source(row // per_device) * per_device + row % per_device
    own_length = lax.dynamic_index_in_dim(cache_lengths, group, 0, keepdims=False)
    places = own_length + token_pos
    cosine, sine = rotary_tables(places, width)
    queries = rotate(
        projected[:, :query_cols].reshape(span, heads_here, width),
        cosine[:, None, :],
        sine[:, None, :],
    ).astype(jnp.bfloat16)
    new_keys = rotate(projected[:, query_cols : query_cols + width], cosine, sine).astype(
        jnp.bfloat16
    )
    new_values = projected[:, query_cols + width : query_cols + 2 * width].astype(jnp.bfloat16)
    hidden = jax.nn.gelu(projected[:, query_cols + 2 * width :], approximate=False).astype(
        jnp.bfloat16
    )
    rows = span * heads_here
    query_rows = queries.reshape(rows, width)

    q_all = lax.all_gather(query_rows, "dp", axis=0, tiled=False)
    q_long = lax.dynamic_index_in_dim(q_all, longest, 0, keepdims=False)
    long_v, long_m, long_s = partial_state(
        q_long, long_keys[:, :width], long_keys[:, width:], (long_pos < long_length)[None, :]
    )
    down_part = jnp.dot(hidden, down_weight, preferred_element_type=jnp.float32)
    short_gath, long_v, long_m, long_s, down_part = lax.optimization_barrier(
        (short_gath, long_v, long_m, long_s, down_part)
    )
    short_keys = spread_from_first(short_gath, "tx").reshape(requests, -1, 2 * width)
    which = jnp.arange(requests, dtype=jnp.int32)
    short_valid = (short_pos[None, :] < cache_lengths[:, None]) & (which != longest)[:, None]
    short_state = partial_state(
        q_all, short_keys[..., :width], short_keys[..., width:], short_valid[:, None, :]
    )
    is_long = which == longest
    state_all = combine(
        short_state,
        (
            jnp.where(is_long[:, None, None], long_v[None], 0.0),
            jnp.where(is_long[:, None], long_m[None], NEGATIVE),
            jnp.where(is_long[:, None], long_s[None], 0.0),
        ),
    )
    packed = jnp.concatenate(
        [state_all[0], state_all[1][..., None], state_all[2][..., None]], axis=-1
    )
    got = lax.all_to_all(packed, "dp", 0, 0, tiled=True)
    part_v, part_m, part_s = got[..., :width], got[..., width], got[..., width + 1]
    best = jnp.max(part_m, axis=0)
    scale = jnp.exp(part_m - best[None])
    state = (
        jnp.sum(part_v * scale[..., None], axis=0),
        best,
        jnp.sum(part_s * scale, axis=0),
    )

    pos_of_row = jnp.repeat(token_pos, heads_here)
    causal = token_pos[None, :] <= pos_of_row[:, None]
    summed, best, total = absorb(state, query_rows, new_keys, new_values, causal)
    attn = (summed / total[:, None]).astype(jnp.bfloat16)
    partial = jnp.dot(attn, dense_weight, preferred_element_type=jnp.float32) + down_part
    layer_rows = scatter_tensor(partial.reshape(n, per_device, width_model))
    return (tokens[0].astype(jnp.float32) + layer_rows).astype(jnp.bfloat16)[None]


def solution(mesh):
    dp = mesh.shape["dp"]
    tensor = mesh.shape["tensor"]
    tx = 4 if tensor % 4 == 0 else 1
    mesh3 = Mesh(mesh.devices.reshape(dp, tx, tensor // tx), ("dp", "tx", "tz"))
    return jax.shard_map(
        local,
        mesh=mesh3,
        in_specs=(
            P("dp", TENSOR, None),
            P(),
            P(),
            P(None, TENSOR),
            P(),
            P(TENSOR, None),
            P(None, TENSOR),
            P(TENSOR, None),
            P(None, TENSOR, "dp", None),
            P(),
        ),
        out_specs=P("dp", TENSOR, None),
        check_vma=False,
    )
```

```python
import math

import jax
import jax.numpy as jnp
from jax import lax
from jax.sharding import Mesh
from jax.sharding import PartitionSpec as P

NEGATIVE = -1e30
TENSOR = ("tx", "tz")


def norm_rows(rows, gain, shift):
    widened = rows.astype(jnp.float32)
    center = jnp.mean(widened, axis=-1, keepdims=True)
    centered = widened - center
    variance = jnp.mean(centered * centered, axis=-1, keepdims=True)
    return (centered * lax.rsqrt(variance + 1e-05) * gain + shift).astype(jnp.bfloat16)


def rotary_tables(places, width):
    half = width // 2
    freqs = jnp.exp(jnp.arange(half, dtype=jnp.float32) * (-2.0 * math.log(10000.0) / width))
    angle = places.astype(jnp.float32)[..., None] * freqs
    cosine = jnp.concatenate([jnp.cos(angle), jnp.cos(angle)], axis=-1)
    sine = jnp.concatenate([jnp.sin(angle), jnp.sin(angle)], axis=-1)
    return (cosine, sine)


def rotate(values, cosine, sine):
    half = values.shape[-1] // 2
    turned = jnp.concatenate([-values[..., half:], values[..., :half]], axis=-1)
    return values * cosine + turned * sine


def combine(first, second):
    first_values, first_top, first_total = first
    second_values, second_top, second_total = second
    best = jnp.maximum(first_top, second_top)
    first_scale = jnp.exp(first_top - best)
    second_scale = jnp.exp(second_top - best)
    return (
        first_values * first_scale[..., None] + second_values * second_scale[..., None],
        best,
        first_total * first_scale + second_total * second_scale,
    )


def absorb(state, queries, key_rows, value_rows, valid):
    scores = jnp.dot(queries, key_rows.T, preferred_element_type=jnp.float32) * (
        1.0 / math.sqrt(queries.shape[-1])
    )
    scores = jnp.where(valid, scores, NEGATIVE)
    best = jnp.max(scores, axis=1)
    weights = jnp.exp(scores - best[:, None])
    block = (
        jnp.dot(weights.astype(jnp.bfloat16), value_rows, preferred_element_type=jnp.float32),
        best,
        jnp.sum(weights, axis=1),
    )
    return combine(state, block)


def fold_keys(state, queries, keys, valid):
    width = queries.shape[-1]
    return absorb(state, queries, keys[:, :width], keys[:, width:], valid)


def empty_state(rows, width, lead):
    return (
        jnp.zeros(lead + (rows, width), jnp.float32),
        jnp.full(lead + (rows,), NEGATIVE, jnp.float32),
        jnp.zeros(lead + (rows,), jnp.float32),
    )


def tensor_index():
    return lax.axis_index("tx") * lax.axis_size("tz") + lax.axis_index("tz")


def bit_reversed(index, bits):
    out = jnp.zeros_like(index)
    for b in range(bits):
        out = out | (((index >> b) & 1) << (bits - 1 - b))
    return out


def round_bits(n):
    bits = n.bit_length() - 1
    low = lax.axis_size("tz").bit_length() - 1
    return list(reversed(range(low))) + list(reversed(range(low, bits)))


def layout_source(index, n):
    order = round_bits(n)
    out = jnp.zeros_like(index)
    for place, b in enumerate(order):
        out = out | (((index >> place) & 1) << b)
    return out


def gather_rounds(piece, n):
    me = tensor_index()
    buf = piece[None]
    for b in round_bits(n):
        other = lax.ppermute(buf, TENSOR, [(i, i ^ (1 << b)) for i in range(n)])
        low = ((me >> b) & 1) == 0
        buf = jnp.concatenate(
            [jnp.where(low, buf, other), jnp.where(low, other, buf)], axis=0
        )
    return buf


def scatter_rounds(partial, n):
    bits = n.bit_length() - 1
    me = tensor_index()
    buf = partial.reshape((2,) * bits + partial.shape[1:])
    for b in reversed(round_bits(n)):
        mine = (me >> b) & 1
        keep = lax.dynamic_index_in_dim(buf, mine, 0, keepdims=False)
        send = lax.dynamic_index_in_dim(buf, 1 - mine, 0, keepdims=False)
        moved = lax.ppermute(
            send.astype(jnp.bfloat16), TENSOR, [(i, i ^ (1 << b)) for i in range(n)]
        )
        buf = keep + moved.astype(jnp.float32)
    return buf


def spread_from_first(x, name):
    size = lax.axis_size(name)
    me = lax.axis_index(name)
    have = 1
    while have < size:
        pairs = [(i, 2 * have - 1 - i) for i in range(have) if 2 * have - 1 - i < size]
        got = lax.ppermute(x, name, pairs)
        x = jnp.where((me >= have) & (me < 2 * have), got, x)
        have *= 2
    return x


def partial_state(queries, keys, values, valid):
    scores = jnp.einsum("...qd,...kd->...qk", queries, keys, preferred_element_type=jnp.float32)
    scores = scores * (1.0 / math.sqrt(queries.shape[-1]))
    scores = jnp.where(valid, scores, NEGATIVE)
    best = jnp.max(scores, axis=-1)
    weights = jnp.exp(scores - best[..., None])
    summed = jnp.einsum(
        "...qk,...kd->...qd",
        weights.astype(jnp.bfloat16),
        values,
        preferred_element_type=jnp.float32,
    )
    return (summed, best, jnp.sum(weights, axis=-1))


SHORT_MAX = 2048


def z_rounds(piece):
    size = lax.axis_size("tz")
    me = lax.axis_index("tz")
    buf = piece[None]
    for b in reversed(range(size.bit_length() - 1)):
        other = lax.ppermute(buf, "tz", [(i, i ^ (1 << b)) for i in range(size)])
        low = ((me >> b) & 1) == 0
        buf = jnp.concatenate(
            [jnp.where(low, buf, other), jnp.where(low, other, buf)], axis=0
        )
    return buf


def gather_tensor(piece):
    nx = lax.axis_size("tx")
    buf = z_rounds(piece)
    wide = jnp.broadcast_to(buf[None], (nx,) + buf.shape)
    return lax.all_to_all(wide, "tx", 0, 0, tiled=True).reshape((-1,) + piece.shape)


def x_spread(buf):
    nx = lax.axis_size("tx")
    wide = jnp.broadcast_to(buf[None], (nx,) + buf.shape)
    return lax.all_to_all(wide, "tx", 0, 0, tiled=True).reshape((-1,) + buf.shape[2:])


def slot_source(index):
    nz = lax.axis_size("tz")
    return (index // nz) * nz + bit_reversed(index % nz, nz.bit_length() - 1)


def scatter_tensor(partial):
    nx, nz = lax.axis_size("tx"), lax.axis_size("tz")
    bits = nz.bit_length() - 1
    buf = partial.reshape((nx, nz) + partial.shape[1:]).astype(jnp.bfloat16)
    over_x = lax.all_to_all(buf, "tx", 0, 0, tiled=True).astype(jnp.float32).sum(0)
    order = [int(format(c, f"0{bits}b")[::-1], 2) if bits else 0 for c in range(nz)]
    ready = jnp.take(over_x, jnp.array(order, dtype=jnp.int32), axis=0).astype(jnp.bfloat16)
    return lax.all_to_all(ready, "tz", 0, 0, tiled=True).astype(jnp.float32).sum(0)


def local(
    tokens,
    ln_gain,
    ln_bias,
    q_weight,
    kv_weight,
    dense_weight,
    up_weight,
    down_weight,
    kv_cache,
    cache_lengths,
):
    n = lax.axis_size("tx") * lax.axis_size("tz")
    width = kv_weight.shape[1] // 2
    query_cols = q_weight.shape[1]
    heads_here = query_cols // width
    width_model = tokens.shape[-1]
    per_device = tokens.shape[1]
    requests, blocks_here, inner_here = kv_cache.shape[:3]
    group = lax.axis_index("dp")
    inner_all = inner_here * lax.axis_size("dp")
    longest = jnp.argmax(cache_lengths).astype(jnp.int32)
    long_length = lax.dynamic_index_in_dim(cache_lengths, longest, 0, keepdims=False)
    inner_pos = group * inner_here + jnp.arange(inner_here, dtype=jnp.int32)

    long_local = lax.dynamic_index_in_dim(kv_cache, longest, 0, keepdims=False)
    normed = norm_rows(tokens[0], ln_gain, ln_bias)
    both = z_rounds(jnp.concatenate([normed.reshape(-1), long_local.reshape(-1)]))
    token_cut = normed.size
    token_all = x_spread(both[:, :token_cut])
    token_all, long_half = lax.optimization_barrier((token_all, both[:, token_cut:]))
    long_all = x_spread(long_half).reshape((n,) + long_local.shape)
    slot_src = slot_source(jnp.arange(n, dtype=jnp.int32))
    long_block = slot_src[:, None] * blocks_here + jnp.arange(blocks_here, dtype=jnp.int32)
    long_pos = (long_block[:, :, None] * inner_all + inner_pos).reshape(-1)
    long_keys = long_all.reshape(-1, 2 * width)

    short_blocks = -(-SHORT_MAX // inner_all)
    short_gath = lax.all_gather(kv_cache, "tz", axis=1, tiled=True)[:, :short_blocks]
    short_pos = (jnp.arange(short_blocks, dtype=jnp.int32)[:, None] * inner_all + inner_pos).reshape(-1)

    piece = token_all.reshape(n * per_device, width_model)
    projected = jnp.concatenate(
        [
            jnp.dot(piece, q_weight, preferred_element_type=jnp.float32),
            jnp.dot(piece, kv_weight, preferred_element_type=jnp.float32),
            jnp.dot(piece, up_weight, preferred_element_type=jnp.float32),
        ],
        axis=1,
    )
    span = projected.shape[0]
    row = jnp.arange(span, dtype=jnp.int32)
    token_pos = slot_source(row // per_device) * per_device + row % per_device
    own_length = lax.dynamic_index_in_dim(cache_lengths, group, 0, keepdims=False)
    places = own_length + token_pos
    cosine, sine = rotary_tables(places, width)
    queries = rotate(
        projected[:, :query_cols].reshape(span, heads_here, width),
        cosine[:, None, :],
        sine[:, None, :],
    ).astype(jnp.bfloat16)
    new_keys = rotate(projected[:, query_cols : query_cols + width], cosine, sine).astype(
        jnp.bfloat16
    )
    new_values = projected[:, query_cols + width : query_cols + 2 * width].astype(jnp.bfloat16)
    hidden = jax.nn.gelu(projected[:, query_cols + 2 * width :], approximate=False).astype(
        jnp.bfloat16
    )
    rows = span * heads_here
    query_rows = queries.reshape(rows, width)

    q_all = lax.all_gather(query_rows, "dp", axis=0, tiled=False)
    q_long = lax.dynamic_index_in_dim(q_all, longest, 0, keepdims=False)
    long_v, long_m, long_s = partial_state(
        q_long, long_keys[:, :width], long_keys[:, width:], (long_pos < long_length)[None, :]
    )
    down_part = jnp.dot(hidden, down_weight, preferred_element_type=jnp.float32)
    short_gath, long_v, long_m, long_s, down_part = lax.optimization_barrier(
        (short_gath, long_v, long_m, long_s, down_part)
    )
    short_keys = spread_from_first(short_gath, "tx").reshape(requests, -1, 2 * width)
    which = jnp.arange(requests, dtype=jnp.int32)
    short_valid = (short_pos[None, :] < cache_lengths[:, None]) & (which != longest)[:, None]
    short_state = partial_state(
        q_all, short_keys[..., :width], short_keys[..., width:], short_valid[:, None, :]
    )
    is_long = which == longest
    state_all = combine(
        short_state,
        (
            jnp.where(is_long[:, None, None], long_v[None], 0.0),
            jnp.where(is_long[:, None], long_m[None], NEGATIVE),
            jnp.where(is_long[:, None], long_s[None], 0.0),
        ),
    )
    packed = jnp.concatenate(
        [state_all[0], state_all[1][..., None], state_all[2][..., None]], axis=-1
    )
    got = lax.all_to_all(packed, "dp", 0, 0, tiled=True)
    part_v, part_m, part_s = got[..., :width], got[..., width], got[..., width + 1]
    best = jnp.max(part_m, axis=0)
    scale = jnp.exp(part_m - best[None])
    state = (
        jnp.sum(part_v * scale[..., None], axis=0),
        best,
        jnp.sum(part_s * scale, axis=0),
    )

    pos_of_row = jnp.repeat(token_pos, heads_here)
    causal = token_pos[None, :] <= pos_of_row[:, None]
    summed, best, total = absorb(state, query_rows, new_keys, new_values, causal)
    attn = (summed / total[:, None]).astype(jnp.bfloat16)
    partial = jnp.dot(attn, dense_weight, preferred_element_type=jnp.float32) + down_part
    layer_rows = scatter_tensor(partial.reshape(n, per_device, width_model))
    return (tokens[0].astype(jnp.float32) + layer_rows).astype(jnp.bfloat16)[None]


def solution(mesh):
    dp = mesh.shape["dp"]
    tensor = mesh.shape["tensor"]
    tx = 4 if tensor % 4 == 0 else 1
    mesh3 = Mesh(mesh.devices.reshape(dp, tx, tensor // tx), ("dp", "tx", "tz"))
    return jax.shard_map(
        local,
        mesh=mesh3,
        in_specs=(
            P("dp", TENSOR, None),
            P(),
            P(),
            P(None, TENSOR),
            P(),
            P(TENSOR, None),
            P(None, TENSOR),
            P(TENSOR, None),
            P(None, TENSOR, "dp", None),
            P(),
        ),
        out_specs=P("dp", TENSOR, None),
        check_vma=False,
    )
```

```python
import math

import jax
import jax.numpy as jnp
from jax import lax
from jax.sharding import Mesh
from jax.sharding import PartitionSpec as P

NEGATIVE = -1e30
TENSOR = ("tx", "tz")


def norm_rows(rows, gain, shift):
    widened = rows.astype(jnp.float32)
    center = jnp.mean(widened, axis=-1, keepdims=True)
    centered = widened - center
    variance = jnp.mean(centered * centered, axis=-1, keepdims=True)
    return (centered * lax.rsqrt(variance + 1e-05) * gain + shift).astype(jnp.bfloat16)


def rotary_tables(places, width):
    half = width // 2
    freqs = jnp.exp(jnp.arange(half, dtype=jnp.float32) * (-2.0 * math.log(10000.0) / width))
    angle = places.astype(jnp.float32)[..., None] * freqs
    cosine = jnp.concatenate([jnp.cos(angle), jnp.cos(angle)], axis=-1)
    sine = jnp.concatenate([jnp.sin(angle), jnp.sin(angle)], axis=-1)
    return (cosine, sine)


def rotate(values, cosine, sine):
    half = values.shape[-1] // 2
    turned = jnp.concatenate([-values[..., half:], values[..., :half]], axis=-1)
    return values * cosine + turned * sine


def combine(first, second):
    first_values, first_top, first_total = first
    second_values, second_top, second_total = second
    best = jnp.maximum(first_top, second_top)
    first_scale = jnp.exp(first_top - best)
    second_scale = jnp.exp(second_top - best)
    return (
        first_values * first_scale[..., None] + second_values * second_scale[..., None],
        best,
        first_total * first_scale + second_total * second_scale,
    )


def absorb(state, queries, key_rows, value_rows, valid):
    scores = jnp.dot(queries, key_rows.T, preferred_element_type=jnp.float32) * (
        1.0 / math.sqrt(queries.shape[-1])
    )
    scores = jnp.where(valid, scores, NEGATIVE)
    best = jnp.max(scores, axis=1)
    weights = jnp.exp(scores - best[:, None])
    block = (
        jnp.dot(weights.astype(jnp.bfloat16), value_rows, preferred_element_type=jnp.float32),
        best,
        jnp.sum(weights, axis=1),
    )
    return combine(state, block)


def fold_keys(state, queries, keys, valid):
    width = queries.shape[-1]
    return absorb(state, queries, keys[:, :width], keys[:, width:], valid)


def empty_state(rows, width, lead):
    return (
        jnp.zeros(lead + (rows, width), jnp.float32),
        jnp.full(lead + (rows,), NEGATIVE, jnp.float32),
        jnp.zeros(lead + (rows,), jnp.float32),
    )


def tensor_index():
    return lax.axis_index("tx") * lax.axis_size("tz") + lax.axis_index("tz")


def bit_reversed(index, bits):
    out = jnp.zeros_like(index)
    for b in range(bits):
        out = out | (((index >> b) & 1) << (bits - 1 - b))
    return out


def round_bits(n):
    bits = n.bit_length() - 1
    low = lax.axis_size("tz").bit_length() - 1
    return list(reversed(range(low))) + list(reversed(range(low, bits)))


def layout_source(index, n):
    order = round_bits(n)
    out = jnp.zeros_like(index)
    for place, b in enumerate(order):
        out = out | (((index >> place) & 1) << b)
    return out


def gather_rounds(piece, n):
    me = tensor_index()
    buf = piece[None]
    for b in round_bits(n):
        other = lax.ppermute(buf, TENSOR, [(i, i ^ (1 << b)) for i in range(n)])
        low = ((me >> b) & 1) == 0
        buf = jnp.concatenate(
            [jnp.where(low, buf, other), jnp.where(low, other, buf)], axis=0
        )
    return buf


def scatter_rounds(partial, n):
    bits = n.bit_length() - 1
    me = tensor_index()
    buf = partial.reshape((2,) * bits + partial.shape[1:])
    for b in reversed(round_bits(n)):
        mine = (me >> b) & 1
        keep = lax.dynamic_index_in_dim(buf, mine, 0, keepdims=False)
        send = lax.dynamic_index_in_dim(buf, 1 - mine, 0, keepdims=False)
        moved = lax.ppermute(
            send.astype(jnp.bfloat16), TENSOR, [(i, i ^ (1 << b)) for i in range(n)]
        )
        buf = keep + moved.astype(jnp.float32)
    return buf


def spread_from_first(x, name):
    size = lax.axis_size(name)
    me = lax.axis_index(name)
    have = 1
    while have < size:
        pairs = [(i, 2 * have - 1 - i) for i in range(have) if 2 * have - 1 - i < size]
        got = lax.ppermute(x, name, pairs)
        x = jnp.where((me >= have) & (me < 2 * have), got, x)
        have *= 2
    return x


def partial_state(queries, keys, values, valid):
    scores = jnp.einsum("...qd,...kd->...qk", queries, keys, preferred_element_type=jnp.float32)
    scores = scores * (1.0 / math.sqrt(queries.shape[-1]))
    scores = jnp.where(valid, scores, NEGATIVE)
    best = jnp.max(scores, axis=-1)
    weights = jnp.exp(scores - best[..., None])
    summed = jnp.einsum(
        "...qk,...kd->...qd",
        weights.astype(jnp.bfloat16),
        values,
        preferred_element_type=jnp.float32,
    )
    return (summed, best, jnp.sum(weights, axis=-1))


SHORT_MAX = 2048


def z_rounds(piece):
    size = lax.axis_size("tz")
    me = lax.axis_index("tz")
    buf = piece[None]
    for b in reversed(range(size.bit_length() - 1)):
        other = lax.ppermute(buf, "tz", [(i, i ^ (1 << b)) for i in range(size)])
        low = ((me >> b) & 1) == 0
        buf = jnp.concatenate(
            [jnp.where(low, buf, other), jnp.where(low, other, buf)], axis=0
        )
    return buf


def gather_tensor(piece):
    nx = lax.axis_size("tx")
    buf = z_rounds(piece)
    wide = jnp.broadcast_to(buf[None], (nx,) + buf.shape)
    return lax.all_to_all(wide, "tx", 0, 0, tiled=True).reshape((-1,) + piece.shape)


def x_spread(buf):
    nx = lax.axis_size("tx")
    wide = jnp.broadcast_to(buf[None], (nx,) + buf.shape)
    return lax.all_to_all(wide, "tx", 0, 0, tiled=True).reshape((-1,) + buf.shape[2:])


def slot_source(index):
    nz = lax.axis_size("tz")
    return (index // nz) * nz + bit_reversed(index % nz, nz.bit_length() - 1)


def scatter_tensor(partial):
    nx, nz = lax.axis_size("tx"), lax.axis_size("tz")
    bits = nz.bit_length() - 1
    buf = partial.reshape((nx, nz) + partial.shape[1:]).astype(jnp.bfloat16)
    over_x = lax.all_to_all(buf, "tx", 0, 0, tiled=True).astype(jnp.float32).sum(0)
    order = [int(format(c, f"0{bits}b")[::-1], 2) if bits else 0 for c in range(nz)]
    ready = jnp.take(over_x, jnp.array(order, dtype=jnp.int32), axis=0).astype(jnp.bfloat16)
    return lax.all_to_all(ready, "tz", 0, 0, tiled=True).astype(jnp.float32).sum(0)


def local(
    tokens,
    ln_gain,
    ln_bias,
    q_weight,
    kv_weight,
    dense_weight,
    up_weight,
    down_weight,
    kv_cache,
    cache_lengths,
):
    n = lax.axis_size("tx") * lax.axis_size("tz")
    width = kv_weight.shape[1] // 2
    query_cols = q_weight.shape[1]
    heads_here = query_cols // width
    width_model = tokens.shape[-1]
    per_device = tokens.shape[1]
    requests, blocks_here, inner_here = kv_cache.shape[:3]
    group = lax.axis_index("dp")
    inner_all = inner_here * lax.axis_size("dp")
    longest = jnp.argmax(cache_lengths).astype(jnp.int32)
    long_length = lax.dynamic_index_in_dim(cache_lengths, longest, 0, keepdims=False)
    inner_pos = group * inner_here + jnp.arange(inner_here, dtype=jnp.int32)
    short_blocks = -(-SHORT_MAX // inner_all)

    long_local = lax.dynamic_index_in_dim(kv_cache, longest, 0, keepdims=False)
    normed = norm_rows(tokens[0], ln_gain, ln_bias)
    both = z_rounds(jnp.concatenate([normed.reshape(-1), long_local.reshape(-1)]))
    token_cut = normed.size
    both, cache_here = lax.optimization_barrier((both, kv_cache))
    short_gath = lax.all_gather(cache_here, "tz", axis=1, tiled=True)[:, :short_blocks]
    token_all = x_spread(both[:, :token_cut])
    token_all, long_half = lax.optimization_barrier((token_all, both[:, token_cut:]))
    long_all = x_spread(long_half).reshape((n,) + long_local.shape)
    slot_src = slot_source(jnp.arange(n, dtype=jnp.int32))
    long_block = slot_src[:, None] * blocks_here + jnp.arange(blocks_here, dtype=jnp.int32)
    long_pos = (long_block[:, :, None] * inner_all + inner_pos).reshape(-1)
    long_keys = long_all.reshape(-1, 2 * width)

    short_pos = (jnp.arange(short_blocks, dtype=jnp.int32)[:, None] * inner_all + inner_pos).reshape(-1)

    piece = token_all.reshape(n * per_device, width_model)
    projected = jnp.concatenate(
        [
            jnp.dot(piece, q_weight, preferred_element_type=jnp.float32),
            jnp.dot(piece, kv_weight, preferred_element_type=jnp.float32),
            jnp.dot(piece, up_weight, preferred_element_type=jnp.float32),
        ],
        axis=1,
    )
    span = projected.shape[0]
    row = jnp.arange(span, dtype=jnp.int32)
    token_pos = slot_source(row // per_device) * per_device + row % per_device
    own_length = lax.dynamic_index_in_dim(cache_lengths, group, 0, keepdims=False)
    places = own_length + token_pos
    cosine, sine = rotary_tables(places, width)
    queries = rotate(
        projected[:, :query_cols].reshape(span, heads_here, width),
        cosine[:, None, :],
        sine[:, None, :],
    ).astype(jnp.bfloat16)
    new_keys = rotate(projected[:, query_cols : query_cols + width], cosine, sine).astype(
        jnp.bfloat16
    )
    new_values = projected[:, query_cols + width : query_cols + 2 * width].astype(jnp.bfloat16)
    hidden = jax.nn.gelu(projected[:, query_cols + 2 * width :], approximate=False).astype(
        jnp.bfloat16
    )
    rows = span * heads_here
    query_rows = queries.reshape(rows, width)

    q_all = lax.all_gather(query_rows, "dp", axis=0, tiled=False)
    q_long = lax.dynamic_index_in_dim(q_all, longest, 0, keepdims=False)
    long_v, long_m, long_s = partial_state(
        q_long, long_keys[:, :width], long_keys[:, width:], (long_pos < long_length)[None, :]
    )
    down_part = jnp.dot(hidden, down_weight, preferred_element_type=jnp.float32)
    short_gath, long_v, long_m, long_s, down_part = lax.optimization_barrier(
        (short_gath, long_v, long_m, long_s, down_part)
    )
    short_keys = spread_from_first(short_gath, "tx").reshape(requests, -1, 2 * width)
    which = jnp.arange(requests, dtype=jnp.int32)
    short_valid = (short_pos[None, :] < cache_lengths[:, None]) & (which != longest)[:, None]
    short_state = partial_state(
        q_all, short_keys[..., :width], short_keys[..., width:], short_valid[:, None, :]
    )
    is_long = which == longest
    state_all = combine(
        short_state,
        (
            jnp.where(is_long[:, None, None], long_v[None], 0.0),
            jnp.where(is_long[:, None], long_m[None], NEGATIVE),
            jnp.where(is_long[:, None], long_s[None], 0.0),
        ),
    )
    packed = jnp.concatenate(
        [state_all[0], state_all[1][..., None], state_all[2][..., None]], axis=-1
    )
    got = lax.all_to_all(packed, "dp", 0, 0, tiled=True)
    part_v, part_m, part_s = got[..., :width], got[..., width], got[..., width + 1]
    best = jnp.max(part_m, axis=0)
    scale = jnp.exp(part_m - best[None])
    state = (
        jnp.sum(part_v * scale[..., None], axis=0),
        best,
        jnp.sum(part_s * scale, axis=0),
    )

    pos_of_row = jnp.repeat(token_pos, heads_here)
    causal = token_pos[None, :] <= pos_of_row[:, None]
    summed, best, total = absorb(state, query_rows, new_keys, new_values, causal)
    attn = (summed / total[:, None]).astype(jnp.bfloat16)
    partial = jnp.dot(attn, dense_weight, preferred_element_type=jnp.float32) + down_part
    layer_rows = scatter_tensor(partial.reshape(n, per_device, width_model))
    return (tokens[0].astype(jnp.float32) + layer_rows).astype(jnp.bfloat16)[None]


def solution(mesh):
    dp = mesh.shape["dp"]
    tensor = mesh.shape["tensor"]
    tx = 4 if tensor % 4 == 0 else 1
    mesh3 = Mesh(mesh.devices.reshape(dp, tx, tensor // tx), ("dp", "tx", "tz"))
    return jax.shard_map(
        local,
        mesh=mesh3,
        in_specs=(
            P("dp", TENSOR, None),
            P(),
            P(),
            P(None, TENSOR),
            P(),
            P(TENSOR, None),
            P(None, TENSOR),
            P(TENSOR, None),
            P(None, TENSOR, "dp", None),
            P(),
        ),
        out_specs=P("dp", TENSOR, None),
        check_vma=False,
    )
```

```python
import math

import jax
import jax.numpy as jnp
from jax import lax
from jax.sharding import Mesh
from jax.sharding import PartitionSpec as P

NEGATIVE = -1e30
TENSOR = ("tx", "tz")


def norm_rows(rows, gain, shift):
    widened = rows.astype(jnp.float32)
    center = jnp.mean(widened, axis=-1, keepdims=True)
    centered = widened - center
    variance = jnp.mean(centered * centered, axis=-1, keepdims=True)
    return (centered * lax.rsqrt(variance + 1e-05) * gain + shift).astype(jnp.bfloat16)


def rotary_tables(places, width):
    half = width // 2
    freqs = jnp.exp(jnp.arange(half, dtype=jnp.float32) * (-2.0 * math.log(10000.0) / width))
    angle = places.astype(jnp.float32)[..., None] * freqs
    cosine = jnp.concatenate([jnp.cos(angle), jnp.cos(angle)], axis=-1)
    sine = jnp.concatenate([jnp.sin(angle), jnp.sin(angle)], axis=-1)
    return (cosine, sine)


def rotate(values, cosine, sine):
    half = values.shape[-1] // 2
    turned = jnp.concatenate([-values[..., half:], values[..., :half]], axis=-1)
    return values * cosine + turned * sine


def combine(first, second):
    first_values, first_top, first_total = first
    second_values, second_top, second_total = second
    best = jnp.maximum(first_top, second_top)
    first_scale = jnp.exp(first_top - best)
    second_scale = jnp.exp(second_top - best)
    return (
        first_values * first_scale[..., None] + second_values * second_scale[..., None],
        best,
        first_total * first_scale + second_total * second_scale,
    )


def absorb(state, queries, key_rows, value_rows, valid):
    scores = jnp.dot(queries, key_rows.T, preferred_element_type=jnp.float32) * (
        1.0 / math.sqrt(queries.shape[-1])
    )
    scores = jnp.where(valid, scores, NEGATIVE)
    best = jnp.max(scores, axis=1)
    weights = jnp.exp(scores - best[:, None])
    block = (
        jnp.dot(weights.astype(jnp.bfloat16), value_rows, preferred_element_type=jnp.float32),
        best,
        jnp.sum(weights, axis=1),
    )
    return combine(state, block)


def fold_keys(state, queries, keys, valid):
    width = queries.shape[-1]
    return absorb(state, queries, keys[:, :width], keys[:, width:], valid)


def empty_state(rows, width, lead):
    return (
        jnp.zeros(lead + (rows, width), jnp.float32),
        jnp.full(lead + (rows,), NEGATIVE, jnp.float32),
        jnp.zeros(lead + (rows,), jnp.float32),
    )


def tensor_index():
    return lax.axis_index("tx") * lax.axis_size("tz") + lax.axis_index("tz")


def bit_reversed(index, bits):
    out = jnp.zeros_like(index)
    for b in range(bits):
        out = out | (((index >> b) & 1) << (bits - 1 - b))
    return out


def round_bits(n):
    bits = n.bit_length() - 1
    low = lax.axis_size("tz").bit_length() - 1
    return list(reversed(range(low))) + list(reversed(range(low, bits)))


def layout_source(index, n):
    order = round_bits(n)
    out = jnp.zeros_like(index)
    for place, b in enumerate(order):
        out = out | (((index >> place) & 1) << b)
    return out


def gather_rounds(piece, n):
    me = tensor_index()
    buf = piece[None]
    for b in round_bits(n):
        other = lax.ppermute(buf, TENSOR, [(i, i ^ (1 << b)) for i in range(n)])
        low = ((me >> b) & 1) == 0
        buf = jnp.concatenate(
            [jnp.where(low, buf, other), jnp.where(low, other, buf)], axis=0
        )
    return buf


def scatter_rounds(partial, n):
    bits = n.bit_length() - 1
    me = tensor_index()
    buf = partial.reshape((2,) * bits + partial.shape[1:])
    for b in reversed(round_bits(n)):
        mine = (me >> b) & 1
        keep = lax.dynamic_index_in_dim(buf, mine, 0, keepdims=False)
        send = lax.dynamic_index_in_dim(buf, 1 - mine, 0, keepdims=False)
        moved = lax.ppermute(
            send.astype(jnp.bfloat16), TENSOR, [(i, i ^ (1 << b)) for i in range(n)]
        )
        buf = keep + moved.astype(jnp.float32)
    return buf


def spread_from_first(x, name):
    size = lax.axis_size(name)
    me = lax.axis_index(name)
    have = 1
    while have < size:
        pairs = [(i, 2 * have - 1 - i) for i in range(have) if 2 * have - 1 - i < size]
        got = lax.ppermute(x, name, pairs)
        x = jnp.where((me >= have) & (me < 2 * have), got, x)
        have *= 2
    return x


def spread_now(x, name):
    me = lax.axis_index(name)
    out = x
    for k in range(1, lax.axis_size(name)):
        out = jnp.where(me == k, lax.ppermute(x, name, [(0, k)]), out)
    return out


def partial_state(queries, keys, values, valid):
    scores = jnp.einsum("...qd,...kd->...qk", queries, keys, preferred_element_type=jnp.float32)
    scores = scores * (1.0 / math.sqrt(queries.shape[-1]))
    scores = jnp.where(valid, scores, NEGATIVE)
    best = jnp.max(scores, axis=-1)
    weights = jnp.exp(scores - best[..., None])
    summed = jnp.einsum(
        "...qk,...kd->...qd",
        weights.astype(jnp.bfloat16),
        values,
        preferred_element_type=jnp.float32,
    )
    return (summed, best, jnp.sum(weights, axis=-1))


SHORT_MAX = 2048


def z_rounds(piece):
    size = lax.axis_size("tz")
    me = lax.axis_index("tz")
    buf = piece[None]
    for b in reversed(range(size.bit_length() - 1)):
        other = lax.ppermute(buf, "tz", [(i, i ^ (1 << b)) for i in range(size)])
        low = ((me >> b) & 1) == 0
        buf = jnp.concatenate(
            [jnp.where(low, buf, other), jnp.where(low, other, buf)], axis=0
        )
    return buf


def gather_tensor(piece):
    nx = lax.axis_size("tx")
    buf = z_rounds(piece)
    wide = jnp.broadcast_to(buf[None], (nx,) + buf.shape)
    return lax.all_to_all(wide, "tx", 0, 0, tiled=True).reshape((-1,) + piece.shape)


def slot_source(index):
    nz = lax.axis_size("tz")
    return (index // nz) * nz + bit_reversed(index % nz, nz.bit_length() - 1)


def scatter_tensor(partial):
    nx, nz = lax.axis_size("tx"), lax.axis_size("tz")
    bits = nz.bit_length() - 1
    buf = partial.reshape((nx, nz) + partial.shape[1:]).astype(jnp.bfloat16)
    over_x = lax.all_to_all(buf, "tx", 0, 0, tiled=True).astype(jnp.float32).sum(0)
    order = [int(format(c, f"0{bits}b")[::-1], 2) if bits else 0 for c in range(nz)]
    ready = jnp.take(over_x, jnp.array(order, dtype=jnp.int32), axis=0).astype(jnp.bfloat16)
    return lax.all_to_all(ready, "tz", 0, 0, tiled=True).astype(jnp.float32).sum(0)


def local(
    tokens,
    ln_gain,
    ln_bias,
    q_weight,
    kv_weight,
    dense_weight,
    up_weight,
    down_weight,
    kv_cache,
    cache_lengths,
):
    n = lax.axis_size("tx") * lax.axis_size("tz")
    width = kv_weight.shape[1] // 2
    query_cols = q_weight.shape[1]
    heads_here = query_cols // width
    width_model = tokens.shape[-1]
    per_device = tokens.shape[1]
    requests, blocks_here, inner_here = kv_cache.shape[:3]
    group = lax.axis_index("dp")
    inner_all = inner_here * lax.axis_size("dp")
    longest = jnp.argmax(cache_lengths).astype(jnp.int32)
    long_length = lax.dynamic_index_in_dim(cache_lengths, longest, 0, keepdims=False)
    inner_pos = group * inner_here + jnp.arange(inner_here, dtype=jnp.int32)

    long_local = lax.dynamic_index_in_dim(kv_cache, longest, 0, keepdims=False)
    normed = norm_rows(tokens[0], ln_gain, ln_bias)
    both = gather_tensor(jnp.concatenate([normed.reshape(-1), long_local.reshape(-1)]))
    token_cut = normed.size
    long_all = both[:, token_cut:].reshape((n,) + long_local.shape)
    slot_src = slot_source(jnp.arange(n, dtype=jnp.int32))
    long_block = slot_src[:, None] * blocks_here + jnp.arange(blocks_here, dtype=jnp.int32)
    long_pos = (long_block[:, :, None] * inner_all + inner_pos).reshape(-1)
    long_keys = long_all.reshape(-1, 2 * width)

    short_blocks = -(-SHORT_MAX // inner_all)
    first_row = spread_now(kv_cache, "tx")
    short_gath = lax.all_gather(first_row, "tz", axis=1, tiled=True)[:, :short_blocks]
    short_pos = (jnp.arange(short_blocks, dtype=jnp.int32)[:, None] * inner_all + inner_pos).reshape(-1)

    piece = both[:, :token_cut].reshape(n * per_device, width_model)
    projected = jnp.concatenate(
        [
            jnp.dot(piece, q_weight, preferred_element_type=jnp.float32),
            jnp.dot(piece, kv_weight, preferred_element_type=jnp.float32),
            jnp.dot(piece, up_weight, preferred_element_type=jnp.float32),
        ],
        axis=1,
    )
    span = projected.shape[0]
    row = jnp.arange(span, dtype=jnp.int32)
    token_pos = slot_source(row // per_device) * per_device + row % per_device
    own_length = lax.dynamic_index_in_dim(cache_lengths, group, 0, keepdims=False)
    places = own_length + token_pos
    cosine, sine = rotary_tables(places, width)
    queries = rotate(
        projected[:, :query_cols].reshape(span, heads_here, width),
        cosine[:, None, :],
        sine[:, None, :],
    ).astype(jnp.bfloat16)
    new_keys = rotate(projected[:, query_cols : query_cols + width], cosine, sine).astype(
        jnp.bfloat16
    )
    new_values = projected[:, query_cols + width : query_cols + 2 * width].astype(jnp.bfloat16)
    hidden = jax.nn.gelu(projected[:, query_cols + 2 * width :], approximate=False).astype(
        jnp.bfloat16
    )
    rows = span * heads_here
    query_rows = queries.reshape(rows, width)

    q_all = lax.all_gather(query_rows, "dp", axis=0, tiled=False)
    q_long = lax.dynamic_index_in_dim(q_all, longest, 0, keepdims=False)
    long_v, long_m, long_s = partial_state(
        q_long, long_keys[:, :width], long_keys[:, width:], (long_pos < long_length)[None, :]
    )
    down_part = jnp.dot(hidden, down_weight, preferred_element_type=jnp.float32)
    short_gath, long_v, long_m, long_s, down_part = lax.optimization_barrier(
        (short_gath, long_v, long_m, long_s, down_part)
    )
    short_keys = short_gath.reshape(requests, -1, 2 * width)
    which = jnp.arange(requests, dtype=jnp.int32)
    short_valid = (short_pos[None, :] < cache_lengths[:, None]) & (which != longest)[:, None]
    short_state = partial_state(
        q_all, short_keys[..., :width], short_keys[..., width:], short_valid[:, None, :]
    )
    is_long = which == longest
    state_all = combine(
        short_state,
        (
            jnp.where(is_long[:, None, None], long_v[None], 0.0),
            jnp.where(is_long[:, None], long_m[None], NEGATIVE),
            jnp.where(is_long[:, None], long_s[None], 0.0),
        ),
    )
    packed = jnp.concatenate(
        [state_all[0], state_all[1][..., None], state_all[2][..., None]], axis=-1
    )
    got = lax.all_to_all(packed, "dp", 0, 0, tiled=True)
    part_v, part_m, part_s = got[..., :width], got[..., width], got[..., width + 1]
    best = jnp.max(part_m, axis=0)
    scale = jnp.exp(part_m - best[None])
    state = (
        jnp.sum(part_v * scale[..., None], axis=0),
        best,
        jnp.sum(part_s * scale, axis=0),
    )

    pos_of_row = jnp.repeat(token_pos, heads_here)
    causal = token_pos[None, :] <= pos_of_row[:, None]
    summed, best, total = absorb(state, query_rows, new_keys, new_values, causal)
    attn = (summed / total[:, None]).astype(jnp.bfloat16)
    partial = jnp.dot(attn, dense_weight, preferred_element_type=jnp.float32) + down_part
    layer_rows = scatter_tensor(partial.reshape(n, per_device, width_model))
    return (tokens[0].astype(jnp.float32) + layer_rows).astype(jnp.bfloat16)[None]


def solution(mesh):
    dp = mesh.shape["dp"]
    tensor = mesh.shape["tensor"]
    tx = 4 if tensor % 4 == 0 else 1
    mesh3 = Mesh(mesh.devices.reshape(dp, tx, tensor // tx), ("dp", "tx", "tz"))
    return jax.shard_map(
        local,
        mesh=mesh3,
        in_specs=(
            P("dp", TENSOR, None),
            P(),
            P(),
            P(None, TENSOR),
            P(),
            P(TENSOR, None),
            P(None, TENSOR),
            P(TENSOR, None),
            P(None, TENSOR, "dp", None),
            P(),
        ),
        out_specs=P("dp", TENSOR, None),
        check_vma=False,
    )
```

```python
import math

import jax
import jax.numpy as jnp
from jax import lax
from jax.sharding import Mesh
from jax.sharding import PartitionSpec as P

NEGATIVE = -1e30
TENSOR = ("tx", "tz")


def norm_rows(rows, gain, shift):
    widened = rows.astype(jnp.float32)
    center = jnp.mean(widened, axis=-1, keepdims=True)
    centered = widened - center
    variance = jnp.mean(centered * centered, axis=-1, keepdims=True)
    return (centered * lax.rsqrt(variance + 1e-05) * gain + shift).astype(jnp.bfloat16)


def rotary_tables(places, width):
    half = width // 2
    freqs = jnp.exp(jnp.arange(half, dtype=jnp.float32) * (-2.0 * math.log(10000.0) / width))
    angle = places.astype(jnp.float32)[..., None] * freqs
    cosine = jnp.concatenate([jnp.cos(angle), jnp.cos(angle)], axis=-1)
    sine = jnp.concatenate([jnp.sin(angle), jnp.sin(angle)], axis=-1)
    return (cosine, sine)


def rotate(values, cosine, sine):
    half = values.shape[-1] // 2
    turned = jnp.concatenate([-values[..., half:], values[..., :half]], axis=-1)
    return values * cosine + turned * sine


def combine(first, second):
    first_values, first_top, first_total = first
    second_values, second_top, second_total = second
    best = jnp.maximum(first_top, second_top)
    first_scale = jnp.exp(first_top - best)
    second_scale = jnp.exp(second_top - best)
    return (
        first_values * first_scale[..., None] + second_values * second_scale[..., None],
        best,
        first_total * first_scale + second_total * second_scale,
    )


def absorb(state, queries, key_rows, value_rows, valid):
    scores = jnp.dot(queries, key_rows.T, preferred_element_type=jnp.float32) * (
        1.0 / math.sqrt(queries.shape[-1])
    )
    scores = jnp.where(valid, scores, NEGATIVE)
    best = jnp.max(scores, axis=1)
    weights = jnp.exp(scores - best[:, None])
    block = (
        jnp.dot(weights.astype(jnp.bfloat16), value_rows, preferred_element_type=jnp.float32),
        best,
        jnp.sum(weights, axis=1),
    )
    return combine(state, block)


def fold_keys(state, queries, keys, valid):
    width = queries.shape[-1]
    return absorb(state, queries, keys[:, :width], keys[:, width:], valid)


def empty_state(rows, width, lead):
    return (
        jnp.zeros(lead + (rows, width), jnp.float32),
        jnp.full(lead + (rows,), NEGATIVE, jnp.float32),
        jnp.zeros(lead + (rows,), jnp.float32),
    )


def tensor_index():
    return lax.axis_index("tx") * lax.axis_size("tz") + lax.axis_index("tz")


def bit_reversed(index, bits):
    out = jnp.zeros_like(index)
    for b in range(bits):
        out = out | (((index >> b) & 1) << (bits - 1 - b))
    return out


def round_bits(n):
    bits = n.bit_length() - 1
    low = lax.axis_size("tz").bit_length() - 1
    return list(reversed(range(low))) + list(reversed(range(low, bits)))


def layout_source(index, n):
    order = round_bits(n)
    out = jnp.zeros_like(index)
    for place, b in enumerate(order):
        out = out | (((index >> place) & 1) << b)
    return out


def gather_rounds(piece, n):
    me = tensor_index()
    buf = piece[None]
    for b in round_bits(n):
        other = lax.ppermute(buf, TENSOR, [(i, i ^ (1 << b)) for i in range(n)])
        low = ((me >> b) & 1) == 0
        buf = jnp.concatenate(
            [jnp.where(low, buf, other), jnp.where(low, other, buf)], axis=0
        )
    return buf


def scatter_rounds(partial, n):
    bits = n.bit_length() - 1
    me = tensor_index()
    buf = partial.reshape((2,) * bits + partial.shape[1:])
    for b in reversed(round_bits(n)):
        mine = (me >> b) & 1
        keep = lax.dynamic_index_in_dim(buf, mine, 0, keepdims=False)
        send = lax.dynamic_index_in_dim(buf, 1 - mine, 0, keepdims=False)
        moved = lax.ppermute(
            send.astype(jnp.bfloat16), TENSOR, [(i, i ^ (1 << b)) for i in range(n)]
        )
        buf = keep + moved.astype(jnp.float32)
    return buf


def spread_from_first(x, name):
    size = lax.axis_size(name)
    me = lax.axis_index(name)
    have = 1
    while have < size:
        pairs = [(i, 2 * have - 1 - i) for i in range(have) if 2 * have - 1 - i < size]
        got = lax.ppermute(x, name, pairs)
        x = jnp.where((me >= have) & (me < 2 * have), got, x)
        have *= 2
    return x


def spread_now(x, name):
    me = lax.axis_index(name)
    out = x
    for k in range(1, lax.axis_size(name)):
        out = jnp.where(me == k, lax.ppermute(x, name, [(0, k)]), out)
    return out


def partial_state(queries, keys, values, valid):
    scores = jnp.einsum("...qd,...kd->...qk", queries, keys, preferred_element_type=jnp.float32)
    scores = scores * (1.0 / math.sqrt(queries.shape[-1]))
    scores = jnp.where(valid, scores, NEGATIVE)
    best = jnp.max(scores, axis=-1)
    weights = jnp.exp(scores - best[..., None])
    summed = jnp.einsum(
        "...qk,...kd->...qd",
        weights.astype(jnp.bfloat16),
        values,
        preferred_element_type=jnp.float32,
    )
    return (summed, best, jnp.sum(weights, axis=-1))


SHORT_MAX = 2048


def z_rounds(piece):
    size = lax.axis_size("tz")
    me = lax.axis_index("tz")
    buf = piece[None]
    for b in reversed(range(size.bit_length() - 1)):
        other = lax.ppermute(buf, "tz", [(i, i ^ (1 << b)) for i in range(size)])
        low = ((me >> b) & 1) == 0
        buf = jnp.concatenate(
            [jnp.where(low, buf, other), jnp.where(low, other, buf)], axis=0
        )
    return buf


def gather_tensor(piece):
    nx = lax.axis_size("tx")
    buf = z_rounds(piece)
    wide = jnp.broadcast_to(buf[None], (nx,) + buf.shape)
    return lax.all_to_all(wide, "tx", 0, 0, tiled=True).reshape((-1,) + piece.shape)


def x_spread(buf):
    nx = lax.axis_size("tx")
    wide = jnp.broadcast_to(buf[None], (nx,) + buf.shape)
    return lax.all_to_all(wide, "tx", 0, 0, tiled=True).reshape((-1,) + buf.shape[1:])


def slot_source(index):
    nz = lax.axis_size("tz")
    return (index // nz) * nz + bit_reversed(index % nz, nz.bit_length() - 1)


def scatter_tensor(partial):
    nx, nz = lax.axis_size("tx"), lax.axis_size("tz")
    bits = nz.bit_length() - 1
    buf = partial.reshape((nx, nz) + partial.shape[1:]).astype(jnp.bfloat16)
    over_x = lax.all_to_all(buf, "tx", 0, 0, tiled=True).astype(jnp.float32).sum(0)
    order = [int(format(c, f"0{bits}b")[::-1], 2) if bits else 0 for c in range(nz)]
    ready = jnp.take(over_x, jnp.array(order, dtype=jnp.int32), axis=0).astype(jnp.bfloat16)
    return lax.all_to_all(ready, "tz", 0, 0, tiled=True).astype(jnp.float32).sum(0)


def local(
    tokens,
    ln_gain,
    ln_bias,
    q_weight,
    kv_weight,
    dense_weight,
    up_weight,
    down_weight,
    kv_cache,
    cache_lengths,
):
    n = lax.axis_size("tx") * lax.axis_size("tz")
    width = kv_weight.shape[1] // 2
    query_cols = q_weight.shape[1]
    heads_here = query_cols // width
    width_model = tokens.shape[-1]
    per_device = tokens.shape[1]
    requests, blocks_here, inner_here = kv_cache.shape[:3]
    group = lax.axis_index("dp")
    inner_all = inner_here * lax.axis_size("dp")
    longest = jnp.argmax(cache_lengths).astype(jnp.int32)
    long_length = lax.dynamic_index_in_dim(cache_lengths, longest, 0, keepdims=False)
    inner_pos = group * inner_here + jnp.arange(inner_here, dtype=jnp.int32)

    long_local = lax.dynamic_index_in_dim(kv_cache, longest, 0, keepdims=False)
    short_blocks = -(-SHORT_MAX // inner_all)
    first_row = spread_now(kv_cache, "tx")
    normed = norm_rows(tokens[0], ln_gain, ln_bias)
    z_part = z_rounds(jnp.concatenate([normed.reshape(-1), long_local.reshape(-1)]))
    z_part, first_row = lax.optimization_barrier((z_part, first_row))
    short_gath = lax.all_gather(first_row, "tz", axis=1, tiled=True)[:, :short_blocks]
    both = x_spread(z_part)
    token_cut = normed.size
    long_all = both[:, token_cut:].reshape((n,) + long_local.shape)
    slot_src = slot_source(jnp.arange(n, dtype=jnp.int32))
    long_block = slot_src[:, None] * blocks_here + jnp.arange(blocks_here, dtype=jnp.int32)
    long_pos = (long_block[:, :, None] * inner_all + inner_pos).reshape(-1)
    long_keys = long_all.reshape(-1, 2 * width)

    short_pos = (jnp.arange(short_blocks, dtype=jnp.int32)[:, None] * inner_all + inner_pos).reshape(-1)

    piece = both[:, :token_cut].reshape(n * per_device, width_model)
    projected = jnp.concatenate(
        [
            jnp.dot(piece, q_weight, preferred_element_type=jnp.float32),
            jnp.dot(piece, kv_weight, preferred_element_type=jnp.float32),
            jnp.dot(piece, up_weight, preferred_element_type=jnp.float32),
        ],
        axis=1,
    )
    span = projected.shape[0]
    row = jnp.arange(span, dtype=jnp.int32)
    token_pos = slot_source(row // per_device) * per_device + row % per_device
    own_length = lax.dynamic_index_in_dim(cache_lengths, group, 0, keepdims=False)
    places = own_length + token_pos
    cosine, sine = rotary_tables(places, width)
    queries = rotate(
        projected[:, :query_cols].reshape(span, heads_here, width),
        cosine[:, None, :],
        sine[:, None, :],
    ).astype(jnp.bfloat16)
    new_keys = rotate(projected[:, query_cols : query_cols + width], cosine, sine).astype(
        jnp.bfloat16
    )
    new_values = projected[:, query_cols + width : query_cols + 2 * width].astype(jnp.bfloat16)
    hidden = jax.nn.gelu(projected[:, query_cols + 2 * width :], approximate=False).astype(
        jnp.bfloat16
    )
    rows = span * heads_here
    query_rows = queries.reshape(rows, width)

    q_all = lax.all_gather(query_rows, "dp", axis=0, tiled=False)
    q_long = lax.dynamic_index_in_dim(q_all, longest, 0, keepdims=False)
    long_v, long_m, long_s = partial_state(
        q_long, long_keys[:, :width], long_keys[:, width:], (long_pos < long_length)[None, :]
    )
    down_part = jnp.dot(hidden, down_weight, preferred_element_type=jnp.float32)
    short_gath, long_v, long_m, long_s, down_part = lax.optimization_barrier(
        (short_gath, long_v, long_m, long_s, down_part)
    )
    short_keys = short_gath.reshape(requests, -1, 2 * width)
    which = jnp.arange(requests, dtype=jnp.int32)
    short_valid = (short_pos[None, :] < cache_lengths[:, None]) & (which != longest)[:, None]
    short_state = partial_state(
        q_all, short_keys[..., :width], short_keys[..., width:], short_valid[:, None, :]
    )
    is_long = which == longest
    state_all = combine(
        short_state,
        (
            jnp.where(is_long[:, None, None], long_v[None], 0.0),
            jnp.where(is_long[:, None], long_m[None], NEGATIVE),
            jnp.where(is_long[:, None], long_s[None], 0.0),
        ),
    )
    packed = jnp.concatenate(
        [state_all[0], state_all[1][..., None], state_all[2][..., None]], axis=-1
    )
    got = lax.all_to_all(packed, "dp", 0, 0, tiled=True)
    part_v, part_m, part_s = got[..., :width], got[..., width], got[..., width + 1]
    best = jnp.max(part_m, axis=0)
    scale = jnp.exp(part_m - best[None])
    state = (
        jnp.sum(part_v * scale[..., None], axis=0),
        best,
        jnp.sum(part_s * scale, axis=0),
    )

    pos_of_row = jnp.repeat(token_pos, heads_here)
    causal = token_pos[None, :] <= pos_of_row[:, None]
    summed, best, total = absorb(state, query_rows, new_keys, new_values, causal)
    attn = (summed / total[:, None]).astype(jnp.bfloat16)
    partial = jnp.dot(attn, dense_weight, preferred_element_type=jnp.float32) + down_part
    layer_rows = scatter_tensor(partial.reshape(n, per_device, width_model))
    return (tokens[0].astype(jnp.float32) + layer_rows).astype(jnp.bfloat16)[None]


def solution(mesh):
    dp = mesh.shape["dp"]
    tensor = mesh.shape["tensor"]
    tx = 4 if tensor % 4 == 0 else 1
    mesh3 = Mesh(mesh.devices.reshape(dp, tx, tensor // tx), ("dp", "tx", "tz"))
    return jax.shard_map(
        local,
        mesh=mesh3,
        in_specs=(
            P("dp", TENSOR, None),
            P(),
            P(),
            P(None, TENSOR),
            P(),
            P(TENSOR, None),
            P(None, TENSOR),
            P(TENSOR, None),
            P(None, TENSOR, "dp", None),
            P(),
        ),
        out_specs=P("dp", TENSOR, None),
        check_vma=False,
    )
```

```python
import math

import jax
import jax.numpy as jnp
from jax import lax
from jax.sharding import Mesh
from jax.sharding import PartitionSpec as P

NEGATIVE = -1e30
TENSOR = ("tx", "tz")


def norm_rows(rows, gain, shift):
    widened = rows.astype(jnp.float32)
    center = jnp.mean(widened, axis=-1, keepdims=True)
    centered = widened - center
    variance = jnp.mean(centered * centered, axis=-1, keepdims=True)
    return (centered * lax.rsqrt(variance + 1e-05) * gain + shift).astype(jnp.bfloat16)


def rotary_tables(places, width):
    half = width // 2
    freqs = jnp.exp(jnp.arange(half, dtype=jnp.float32) * (-2.0 * math.log(10000.0) / width))
    angle = places.astype(jnp.float32)[..., None] * freqs
    cosine = jnp.concatenate([jnp.cos(angle), jnp.cos(angle)], axis=-1)
    sine = jnp.concatenate([jnp.sin(angle), jnp.sin(angle)], axis=-1)
    return (cosine, sine)


def rotate(values, cosine, sine):
    half = values.shape[-1] // 2
    turned = jnp.concatenate([-values[..., half:], values[..., :half]], axis=-1)
    return values * cosine + turned * sine


def combine(first, second):
    first_values, first_top, first_total = first
    second_values, second_top, second_total = second
    best = jnp.maximum(first_top, second_top)
    first_scale = jnp.exp(first_top - best)
    second_scale = jnp.exp(second_top - best)
    return (
        first_values * first_scale[..., None] + second_values * second_scale[..., None],
        best,
        first_total * first_scale + second_total * second_scale,
    )


def absorb(state, queries, key_rows, value_rows, valid):
    scores = jnp.dot(queries, key_rows.T, preferred_element_type=jnp.float32) * (
        1.0 / math.sqrt(queries.shape[-1])
    )
    scores = jnp.where(valid, scores, NEGATIVE)
    best = jnp.max(scores, axis=1)
    weights = jnp.exp(scores - best[:, None])
    block = (
        jnp.dot(weights.astype(jnp.bfloat16), value_rows, preferred_element_type=jnp.float32),
        best,
        jnp.sum(weights, axis=1),
    )
    return combine(state, block)


def fold_keys(state, queries, keys, valid):
    width = queries.shape[-1]
    return absorb(state, queries, keys[:, :width], keys[:, width:], valid)


def empty_state(rows, width, lead):
    return (
        jnp.zeros(lead + (rows, width), jnp.float32),
        jnp.full(lead + (rows,), NEGATIVE, jnp.float32),
        jnp.zeros(lead + (rows,), jnp.float32),
    )


def tensor_index():
    return lax.axis_index("tx") * lax.axis_size("tz") + lax.axis_index("tz")


def bit_reversed(index, bits):
    out = jnp.zeros_like(index)
    for b in range(bits):
        out = out | (((index >> b) & 1) << (bits - 1 - b))
    return out


def round_bits(n):
    bits = n.bit_length() - 1
    low = lax.axis_size("tz").bit_length() - 1
    return list(reversed(range(low))) + list(reversed(range(low, bits)))


def layout_source(index, n):
    order = round_bits(n)
    out = jnp.zeros_like(index)
    for place, b in enumerate(order):
        out = out | (((index >> place) & 1) << b)
    return out


def gather_rounds(piece, n):
    me = tensor_index()
    buf = piece[None]
    for b in round_bits(n):
        other = lax.ppermute(buf, TENSOR, [(i, i ^ (1 << b)) for i in range(n)])
        low = ((me >> b) & 1) == 0
        buf = jnp.concatenate(
            [jnp.where(low, buf, other), jnp.where(low, other, buf)], axis=0
        )
    return buf


def scatter_rounds(partial, n):
    bits = n.bit_length() - 1
    me = tensor_index()
    buf = partial.reshape((2,) * bits + partial.shape[1:])
    for b in reversed(round_bits(n)):
        mine = (me >> b) & 1
        keep = lax.dynamic_index_in_dim(buf, mine, 0, keepdims=False)
        send = lax.dynamic_index_in_dim(buf, 1 - mine, 0, keepdims=False)
        moved = lax.ppermute(
            send.astype(jnp.bfloat16), TENSOR, [(i, i ^ (1 << b)) for i in range(n)]
        )
        buf = keep + moved.astype(jnp.float32)
    return buf


def spread_from_first(x, name):
    size = lax.axis_size(name)
    me = lax.axis_index(name)
    have = 1
    while have < size:
        pairs = [(i, 2 * have - 1 - i) for i in range(have) if 2 * have - 1 - i < size]
        got = lax.ppermute(x, name, pairs)
        x = jnp.where((me >= have) & (me < 2 * have), got, x)
        have *= 2
    return x


def spread_now(x, name):
    me = lax.axis_index(name)
    out = x
    for k in range(1, lax.axis_size(name)):
        out = jnp.where(me == k, lax.ppermute(x, name, [(0, k)]), out)
    return out


def partial_state(queries, keys, values, valid):
    scores = jnp.einsum("...qd,...kd->...qk", queries, keys, preferred_element_type=jnp.float32)
    scores = scores * (1.0 / math.sqrt(queries.shape[-1]))
    scores = jnp.where(valid, scores, NEGATIVE)
    best = jnp.max(scores, axis=-1)
    weights = jnp.exp(scores - best[..., None])
    summed = jnp.einsum(
        "...qk,...kd->...qd",
        weights.astype(jnp.bfloat16),
        values,
        preferred_element_type=jnp.float32,
    )
    return (summed, best, jnp.sum(weights, axis=-1))


SHORT_MAX = 2048


def z_rounds(piece):
    size = lax.axis_size("tz")
    me = lax.axis_index("tz")
    buf = piece[None]
    for b in reversed(range(size.bit_length() - 1)):
        other = lax.ppermute(buf, "tz", [(i, i ^ (1 << b)) for i in range(size)])
        low = ((me >> b) & 1) == 0
        buf = jnp.concatenate(
            [jnp.where(low, buf, other), jnp.where(low, other, buf)], axis=0
        )
    return buf


def gather_tensor(piece):
    nx = lax.axis_size("tx")
    buf = z_rounds(piece)
    wide = jnp.broadcast_to(buf[None], (nx,) + buf.shape)
    return lax.all_to_all(wide, "tx", 0, 0, tiled=True).reshape((-1,) + piece.shape)


def x_spread(buf):
    nx = lax.axis_size("tx")
    wide = jnp.broadcast_to(buf[None], (nx,) + buf.shape)
    return lax.all_to_all(wide, "tx", 0, 0, tiled=True).reshape((-1,) + buf.shape[1:])


def slot_source(index):
    nz = lax.axis_size("tz")
    return (index // nz) * nz + bit_reversed(index % nz, nz.bit_length() - 1)


def scatter_tensor(partial):
    nx, nz = lax.axis_size("tx"), lax.axis_size("tz")
    bits = nz.bit_length() - 1
    buf = partial.reshape((nx, nz) + partial.shape[1:]).astype(jnp.bfloat16)
    over_x = lax.all_to_all(buf, "tx", 0, 0, tiled=True).astype(jnp.float32).sum(0)
    order = [int(format(c, f"0{bits}b")[::-1], 2) if bits else 0 for c in range(nz)]
    ready = jnp.take(over_x, jnp.array(order, dtype=jnp.int32), axis=0).astype(jnp.bfloat16)
    return lax.all_to_all(ready, "tz", 0, 0, tiled=True).astype(jnp.float32).sum(0)


def local(
    tokens,
    ln_gain,
    ln_bias,
    q_weight,
    kv_weight,
    dense_weight,
    up_weight,
    down_weight,
    kv_cache,
    cache_lengths,
):
    n = lax.axis_size("tx") * lax.axis_size("tz")
    width = kv_weight.shape[1] // 2
    query_cols = q_weight.shape[1]
    heads_here = query_cols // width
    width_model = tokens.shape[-1]
    per_device = tokens.shape[1]
    requests, blocks_here, inner_here = kv_cache.shape[:3]
    group = lax.axis_index("dp")
    inner_all = inner_here * lax.axis_size("dp")
    longest = jnp.argmax(cache_lengths).astype(jnp.int32)
    long_length = lax.dynamic_index_in_dim(cache_lengths, longest, 0, keepdims=False)
    inner_pos = group * inner_here + jnp.arange(inner_here, dtype=jnp.int32)

    long_local = lax.dynamic_index_in_dim(kv_cache, longest, 0, keepdims=False)
    short_blocks = -(-SHORT_MAX // inner_all)
    first_row = spread_now(kv_cache, "tx")
    normed = norm_rows(tokens[0], ln_gain, ln_bias)
    z_part = z_rounds(jnp.concatenate([normed.reshape(-1), long_local.reshape(-1)]))
    z_part, first_row = lax.optimization_barrier((z_part, first_row))
    short_gath = lax.all_gather(first_row, "tz", axis=1, tiled=True)[:, :short_blocks]
    both = x_spread(z_part)
    token_cut = normed.size
    long_all = both[:, token_cut:].reshape((n,) + long_local.shape)
    slot_src = slot_source(jnp.arange(n, dtype=jnp.int32))
    long_block = slot_src[:, None] * blocks_here + jnp.arange(blocks_here, dtype=jnp.int32)
    long_pos = (long_block[:, :, None] * inner_all + inner_pos).reshape(-1)
    long_keys = long_all.reshape(-1, 2 * width)

    short_pos = (jnp.arange(short_blocks, dtype=jnp.int32)[:, None] * inner_all + inner_pos).reshape(-1)

    piece = both[:, :token_cut].reshape(n * per_device, width_model)
    projected = jnp.concatenate(
        [
            jnp.dot(piece, q_weight, preferred_element_type=jnp.float32),
            jnp.dot(piece, kv_weight, preferred_element_type=jnp.float32),
            jnp.dot(piece, up_weight, preferred_element_type=jnp.float32),
        ],
        axis=1,
    )
    span = projected.shape[0]
    row = jnp.arange(span, dtype=jnp.int32)
    token_pos = slot_source(row // per_device) * per_device + row % per_device
    own_length = lax.dynamic_index_in_dim(cache_lengths, group, 0, keepdims=False)
    places = own_length + token_pos
    cosine, sine = rotary_tables(places, width)
    queries = rotate(
        projected[:, :query_cols].reshape(span, heads_here, width),
        cosine[:, None, :],
        sine[:, None, :],
    ).astype(jnp.bfloat16)
    new_keys = rotate(projected[:, query_cols : query_cols + width], cosine, sine).astype(
        jnp.bfloat16
    )
    new_values = projected[:, query_cols + width : query_cols + 2 * width].astype(jnp.bfloat16)
    hidden = jax.nn.gelu(projected[:, query_cols + 2 * width :], approximate=False).astype(
        jnp.bfloat16
    )
    rows = span * heads_here
    query_rows = queries.reshape(rows, width)

    q_all = lax.all_gather(query_rows, "dp", axis=0, tiled=False)
    q_long = lax.dynamic_index_in_dim(q_all, longest, 0, keepdims=False)
    long_v, long_m, long_s = partial_state(
        q_long, long_keys[:, :width], long_keys[:, width:], (long_pos < long_length)[None, :]
    )
    down_part = jnp.dot(hidden, down_weight, preferred_element_type=jnp.float32)
    pos_of_row = jnp.repeat(token_pos, heads_here)
    causal = token_pos[None, :] <= pos_of_row[:, None]
    fresh = partial_state(query_rows, new_keys, new_values, causal)
    short_gath, long_v, long_m, long_s, down_part, fresh = lax.optimization_barrier(
        (short_gath, long_v, long_m, long_s, down_part, fresh)
    )
    short_keys = short_gath.reshape(requests, -1, 2 * width)
    which = jnp.arange(requests, dtype=jnp.int32)
    short_valid = (short_pos[None, :] < cache_lengths[:, None]) & (which != longest)[:, None]
    short_state = partial_state(
        q_all, short_keys[..., :width], short_keys[..., width:], short_valid[:, None, :]
    )
    is_long = which == longest
    state_all = combine(
        short_state,
        (
            jnp.where(is_long[:, None, None], long_v[None], 0.0),
            jnp.where(is_long[:, None], long_m[None], NEGATIVE),
            jnp.where(is_long[:, None], long_s[None], 0.0),
        ),
    )
    packed = jnp.concatenate(
        [state_all[0], state_all[1][..., None], state_all[2][..., None]], axis=-1
    )
    got = lax.all_to_all(packed, "dp", 0, 0, tiled=True)
    part_v, part_m, part_s = got[..., :width], got[..., width], got[..., width + 1]
    best = jnp.max(part_m, axis=0)
    scale = jnp.exp(part_m - best[None])
    state = (
        jnp.sum(part_v * scale[..., None], axis=0),
        best,
        jnp.sum(part_s * scale, axis=0),
    )

    summed, best, total = combine(state, fresh)
    attn = (summed / total[:, None]).astype(jnp.bfloat16)
    partial = jnp.dot(attn, dense_weight, preferred_element_type=jnp.float32) + down_part
    layer_rows = scatter_tensor(partial.reshape(n, per_device, width_model))
    return (tokens[0].astype(jnp.float32) + layer_rows).astype(jnp.bfloat16)[None]


def solution(mesh):
    dp = mesh.shape["dp"]
    tensor = mesh.shape["tensor"]
    tx = 4 if tensor % 4 == 0 else 1
    mesh3 = Mesh(mesh.devices.reshape(dp, tx, tensor // tx), ("dp", "tx", "tz"))
    return jax.shard_map(
        local,
        mesh=mesh3,
        in_specs=(
            P("dp", TENSOR, None),
            P(),
            P(),
            P(None, TENSOR),
            P(),
            P(TENSOR, None),
            P(None, TENSOR),
            P(TENSOR, None),
            P(None, TENSOR, "dp", None),
            P(),
        ),
        out_specs=P("dp", TENSOR, None),
        check_vma=False,
    )
```
